512 devices in a mesh: chan: 32 (over z, x_hi), seg: 16 (over y, x_lo, core).
Axes of the slice: x: 4 (x_hi: 2, x_lo: 2; x = x_hi * 2 + x_lo), y: 4, z: 16, core: 2. Of those that a mesh axis runs over, the one named last changes fastest.
Arguments:
- traces: bfloat16 [512, 16, 384], P('chan', 'seg')
- taper_len: int32 [512], P('chan'), may hold values from 1 to 192
- gather_id: int32 [512, 512], P('chan'), may hold values from 0 to 511, as said below
- offset_bin: int32 [512, 512], P('chan'), may hold values from 0 to 1, as said below
Outputs:
- stack: float32 [512, 2, 256], P(('chan', 'seg'))
The draws below stay inside these ranges and needn't reach their ends.
Inputs may be any that keep to these rules, and one draw needn't show every extreme that they name: Channels lie on a fiber at integer positions p_0 < p_1 < ... with steps of 2 to 5; gather_id[i, j] = floor((p_i + p_j - 2 p_0) * 512 / (2 (p_last - p_0) + 1)). offset_bin[i, j] = floor(|p_i - p_j| * 2 / (p_last - p_0 + 1)) with the same positions.
All inputs are finite; a program needn't handle non-finite values.
Results may differ from the reference program's by a relative error of at most 0.0039.
Values may be sent and summed in bfloat16 or wider, within the bound.
No kernel may reach another device: no remote copies, remote signals or barrier semaphores. Data moves between devices by JAX's collectives and lax.ppermute only.
A program may use at most 64 MiB of HBM per device.

```python
import math
import jax
import jax.numpy as jnp
from jax import lax

CH_DEV = 16
SAMP = 384
LAGS = 256
OFFBINS = 2
CHANNELS = 512
SEGMENTS = 16
GATHERS = 512
N_CHAN = 32


def draw_traces(key, part):
    key_scale, key_noise = jax.random.split(key, 2)
    shape = (CHANNELS, SEGMENTS, SAMP)
    scales = jnp.exp(jax.random.uniform(key_scale, (CHANNELS, SEGMENTS, 1), jnp.float32, math.log(0.3), math.log(3.0)))
    values = scales * jax.random.normal(key_noise, shape, jnp.float32)
    return values.astype(jnp.bfloat16)


def fiber_positions(key):
    spacing = jax.random.randint(jax.random.fold_in(key, 7), (CHANNELS,), 2, 6)
    return jnp.cumsum(spacing).astype(jnp.int32)


def draw_gather_id(key, part):
    places = fiber_positions(key)
    span = places[-1] - places[0]
    middle = places[:, None] + places[None, :] - 2 * places[0]
    return (middle * GATHERS // (2 * span + 1)).astype(jnp.int32)


def draw_offset_bin(key, part):
    places = fiber_positions(key)
    span = places[-1] - places[0]
    distance = jnp.abs(places[:, None] - places[None, :])
    return (distance * OFFBINS // (span + 1)).astype(jnp.int32)


def with_ends(values, own_key, low, high):
    place = [jax.random.randint(jax.random.fold_in(own_key, axis), (), 0, length) for axis, length in enumerate(values.shape)]
    main_axis = values.shape.index(max(values.shape))
    beside = place[:main_axis] + [(place[main_axis] + 1) % values.shape[main_axis]] + place[main_axis + 1:]
    return values.at[tuple(place)].set(low).at[tuple(beside)].set(high)


def setup_inputs(seed: int = 0) -> dict:
    streams_of = jax.random.split(jax.random.key(seed), 5)
    traces = draw_traces(jax.random.fold_in(streams_of[4], 71), 0)
    taper_len = with_ends(jax.random.randint(streams_of[1], (CHANNELS,), 1, SAMP // 2 + 1), jax.random.fold_in(streams_of[1], 1), 1, (SAMP // 2 + 1) - 1).astype(jnp.int32)
    gather_id = draw_gather_id(jax.random.fold_in(streams_of[4], 71), 0)
    offset_bin = draw_offset_bin(jax.random.fold_in(streams_of[4], 71), 0)
    return {"traces": traces, "taper_len": taper_len, "gather_id": gather_id, "offset_bin": offset_bin}


def normalize(traces, taper_len):
    values = traces.astype(jnp.float32)
    sample_count = values.shape[2]
    power = lax.optimization_barrier(jnp.mean(values * values, axis=2, keepdims=True))
    times = jnp.arange(sample_count).astype(jnp.float32)
    length = taper_len.astype(jnp.float32)[:, None, None]
    window = jnp.minimum(1.0, jnp.minimum((times + 1.0) / length, (sample_count - times) / length))
    return (window * values * lax.rsqrt(power + 1e-06)).astype(jnp.bfloat16)

def hankel(normed, lag_count):
    chan_count, seg_count, sample_count = normed.shape
    shifts = jnp.arange(lag_count, dtype=jnp.int32) - lag_count // 2
    source = jnp.arange(sample_count, dtype=jnp.int32)[:, None] - shifts[None, :]
    inside = (source >= 0) & (source < sample_count)
    picked = jnp.take(normed, jnp.clip(source, 0, sample_count - 1), axis=2)
    picked = jnp.where(inside, picked, jnp.zeros((), normed.dtype))
    return jnp.transpose(picked, (1, 2, 0, 3)).reshape(seg_count * sample_count, chan_count * lag_count)

def reference(traces, taper_len, gather_id, offset_bin):
    normed = normalize(traces, taper_len)
    flat = normed.reshape(CHANNELS, SEGMENTS * SAMP)
    bucket_count = GATHERS * OFFBINS
    labels_all = gather_id * OFFBINS + offset_bin
    rows_all = jnp.arange(CHANNELS, dtype=jnp.int32)
    labels_all = jnp.where(rows_all[:, None] == rows_all[None, :], bucket_count, labels_all).astype(jnp.int32)
    blocks = normed.reshape(N_CHAN, CH_DEV, SEGMENTS, SAMP)
    label_blocks = labels_all.reshape(N_CHAN, CH_DEV, CHANNELS)

    def step(total, inputs):
        block, labels = inputs
        kernel = hankel(block, LAGS)
        product = jnp.dot(flat, kernel, preferred_element_type=jnp.float32).reshape(CHANNELS * CH_DEV, LAGS)
        return (total.at[jnp.transpose(labels).reshape(-1)].add(product, mode='drop'), None)
    total, unused = lax.scan(step, jnp.zeros((bucket_count, LAGS), jnp.float32), (blocks, label_blocks))
    return (total * (1.0 / math.sqrt(SAMP * SEGMENTS))).reshape(GATHERS, OFFBINS, LAGS)
```

```python
import math

import jax
import jax.numpy as jnp
from jax import lax
from jax.sharding import PartitionSpec as P

LAGS = 256
OFFBINS = 2


def normalize(traces, taper_len):
    values = traces.astype(jnp.float32)
    sample_count = values.shape[2]
    power = jnp.mean(values * values, axis=2, keepdims=True)
    times = jnp.arange(sample_count).astype(jnp.float32)
    length = taper_len.astype(jnp.float32)[:, None, None]
    window = jnp.minimum(1.0, jnp.minimum((times + 1.0) / length, (sample_count - times) / length))
    return (window * values * lax.rsqrt(power + 1e-06)).astype(jnp.bfloat16)


def hankel(normed, lag_count):
    chan_count, seg_count, sample_count = normed.shape
    turned = jnp.transpose(normed, (1, 2, 0))
    padded = jnp.pad(turned, ((0, 0), (lag_count // 2, lag_count // 2), (0, 0)))
    slices = [padded[:, lag_count - k : lag_count - k + sample_count, :] for k in range(lag_count)]
    picked = jnp.stack(slices, axis=3)
    return picked.reshape(seg_count * sample_count, chan_count * lag_count)


def shards(traces, taper_len, gather_id, offset_bin):
    chan_count = traces.shape[0]
    chan_devices = lax.axis_size("chan")
    seg_devices = lax.axis_size("seg")
    bucket_count = chan_devices * seg_devices * OFFBINS
    normed = normalize(traces, taper_len)
    kernel = hankel(normed, LAGS)
    first_row = lax.axis_index("chan") * chan_count
    own_rows = first_row + jnp.arange(chan_count, dtype=jnp.int32)[None, :]
    empty = jnp.zeros((bucket_count, LAGS), jnp.float32)
    flat = lax.optimization_barrier(normed.reshape(chan_count, -1))
    piece = lax.all_gather(flat, "chan", axis=0, tiled=True)
    row_count = piece.shape[0]
    product = jnp.dot(piece, kernel, preferred_element_type=jnp.float32)
    product = product.reshape(row_count * chan_count, LAGS)
    labels = jnp.transpose(gather_id * OFFBINS + offset_bin)
    partner = jnp.arange(row_count, dtype=jnp.int32)[:, None]
    labels = jnp.where(partner == own_rows, bucket_count, labels).reshape(-1)
    total = empty.at[labels].add(product, mode="drop")
    scale = 1.0 / math.sqrt(traces.shape[2] * traces.shape[1] * seg_devices)
    stacked = (total * scale).reshape(chan_devices, seg_devices, OFFBINS, LAGS)
    stacked = jnp.transpose(stacked, (1, 0, 2, 3))
    part = lax.psum_scatter(stacked, "seg", scatter_dimension=0, tiled=True)
    part = part.reshape(chan_devices, OFFBINS, LAGS)
    result = lax.psum_scatter(part, "chan", scatter_dimension=0, tiled=True)
    return result


def solution(mesh):
    placed = (P("chan", "seg", None), P("chan"), P("chan", None), P("chan", None))
    return jax.shard_map(
        shards,
        mesh=mesh,
        in_specs=placed,
        out_specs=P(("chan", "seg"), None, None),
        check_vma=False,
    )
```

```python
import math

import jax
import jax.numpy as jnp
from jax import lax
from jax.sharding import PartitionSpec as P

LAGS = 256
OFFBINS = 2


def normalize(traces, taper_len):
    values = traces.astype(jnp.float32)
    sample_count = values.shape[2]
    power = jnp.mean(values * values, axis=2, keepdims=True)
    times = jnp.arange(sample_count).astype(jnp.float32)
    length = taper_len.astype(jnp.float32)[:, None, None]
    window = jnp.minimum(1.0, jnp.minimum((times + 1.0) / length, (sample_count - times) / length))
    return (window * values * lax.rsqrt(power + 1e-06)).astype(jnp.bfloat16)


def hankel(normed, lag_count):
    chan_count, seg_count, sample_count = normed.shape
    turned = jnp.transpose(normed, (1, 2, 0))
    padded = jnp.pad(turned, ((0, 0), (lag_count // 2, lag_count // 2), (0, 0)))
    slices = [padded[:, lag_count - k : lag_count - k + sample_count, :] for k in range(lag_count)]
    picked = jnp.stack(slices, axis=3)
    return picked.reshape(seg_count * sample_count, chan_count * lag_count)


def shards(traces, taper_len, gather_id, offset_bin):
    chan_count = traces.shape[0]
    chan_devices = lax.axis_size("chan")
    seg_devices = lax.axis_size("seg")
    bucket_count = chan_devices * seg_devices * OFFBINS
    normed = normalize(traces, taper_len)
    kernel = hankel(normed, LAGS)
    first_row = lax.axis_index("chan") * chan_count
    own_rows = first_row + jnp.arange(chan_count, dtype=jnp.int32)[None, :]
    empty = jnp.zeros((bucket_count, LAGS), jnp.float32)
    flat = lax.optimization_barrier(normed.reshape(chan_count, -1))
    copies = jnp.broadcast_to(flat[None], (chan_devices,) + flat.shape)
    piece = lax.all_to_all(copies, "chan", 0, 0, tiled=True).reshape(-1, flat.shape[1])
    row_count = piece.shape[0]
    product = jnp.dot(piece, kernel, preferred_element_type=jnp.float32)
    product = product.reshape(row_count * chan_count, LAGS)
    labels = jnp.transpose(gather_id * OFFBINS + offset_bin)
    partner = jnp.arange(row_count, dtype=jnp.int32)[:, None]
    labels = jnp.where(partner == own_rows, bucket_count, labels).reshape(-1)
    total = empty.at[labels].add(product, mode="drop")
    scale = 1.0 / math.sqrt(traces.shape[2] * traces.shape[1] * seg_devices)
    stacked = (total * scale).reshape(chan_devices, seg_devices, OFFBINS, LAGS)
    stacked = jnp.transpose(stacked, (1, 0, 2, 3))
    part = lax.psum_scatter(stacked, "seg", scatter_dimension=0, tiled=True)
    part = part.reshape(chan_devices, OFFBINS, LAGS)
    pieces = lax.all_to_all(part, "chan", 0, 0, tiled=True)
    return jnp.sum(pieces, axis=0, keepdims=True)


def solution(mesh):
    placed = (P("chan", "seg", None), P("chan"), P("chan", None), P("chan", None))
    return jax.shard_map(
        shards,
        mesh=mesh,
        in_specs=placed,
        out_specs=P(("chan", "seg"), None, None),
        check_vma=False,
    )
```

```python
import math

import jax
import jax.numpy as jnp
from jax import lax
from jax.sharding import PartitionSpec as P

LAGS = 256
OFFBINS = 2


def normalize(traces, taper_len):
    values = traces.astype(jnp.float32)
    sample_count = values.shape[2]
    power = jnp.mean(values * values, axis=2, keepdims=True)
    times = jnp.arange(sample_count).astype(jnp.float32)
    length = taper_len.astype(jnp.float32)[:, None, None]
    window = jnp.minimum(1.0, jnp.minimum((times + 1.0) / length, (sample_count - times) / length))
    return (window * values * lax.rsqrt(power + 1e-06)).astype(jnp.bfloat16)


def hankel(normed, lag_count):
    chan_count, seg_count, sample_count = normed.shape
    turned = jnp.transpose(normed, (1, 2, 0))
    padded = jnp.pad(turned, ((0, 0), (lag_count // 2, lag_count // 2), (0, 0)))
    slices = [padded[:, lag_count - k : lag_count - k + sample_count, :] for k in range(lag_count)]
    picked = jnp.stack(slices, axis=3)
    return picked.reshape(seg_count * sample_count, chan_count * lag_count)


def shards(traces, taper_len, gather_id, offset_bin):
    chan_count = traces.shape[0]
    chan_devices = lax.axis_size("chan")
    seg_devices = lax.axis_size("seg")
    bucket_count = chan_devices * seg_devices * OFFBINS
    normed = normalize(traces, taper_len)
    kernel = hankel(normed, LAGS)
    first_row = lax.axis_index("chan") * chan_count
    own_rows = first_row + jnp.arange(chan_count, dtype=jnp.int32)[None, :]
    flat = lax.optimization_barrier(normed.reshape(chan_count, -1))
    copies = jnp.broadcast_to(flat[None], (chan_devices,) + flat.shape)
    piece = lax.all_to_all(copies, "chan", 0, 0, tiled=True).reshape(-1, flat.shape[1])
    row_count = piece.shape[0]
    product = jnp.dot(piece, kernel, preferred_element_type=jnp.float32)
    product = product.reshape(row_count * chan_count, LAGS)
    labels = jnp.transpose(gather_id * OFFBINS + offset_bin)
    partner = jnp.arange(row_count, dtype=jnp.int32)[:, None]
    labels = jnp.where(partner == own_rows, -1, labels).reshape(-1)
    gathers = chan_devices * seg_devices
    low_span = 2 * (row_count - 1)
    reach = (low_span + 5 * (chan_count - 1)) * gathers // (2 * low_span + 1) + 2
    depth = -(-(reach - 1) // seg_devices) + 1
    depth = -(-depth // 8) * 8
    start = gather_id[0, 0]
    lanes = jnp.arange(seg_devices, dtype=jnp.int32)
    first = jnp.minimum((start - lanes + seg_devices - 1) // seg_devices, chan_devices - depth)
    first = jnp.maximum(first, 0)
    window = (first[:, None] + jnp.arange(depth, dtype=jnp.int32)[None, :]) * seg_devices + lanes[:, None]
    wanted = (window[:, :, None] * OFFBINS + jnp.arange(OFFBINS, dtype=jnp.int32)).reshape(-1)
    onehot = (wanted[:, None] == labels[None, :]).astype(jnp.bfloat16)
    high = product.astype(jnp.bfloat16)
    low = (product - high.astype(jnp.float32)).astype(jnp.bfloat16)
    both = jnp.dot(onehot, jnp.concatenate([high, low], axis=1), preferred_element_type=jnp.float32)
    total = both[:, :LAGS] + both[:, LAGS:]
    scale = 1.0 / math.sqrt(traces.shape[2] * traces.shape[1] * seg_devices)
    stacked = (total * scale).reshape(seg_devices, depth, OFFBINS, LAGS)
    part = lax.psum_scatter(stacked, "seg", scatter_dimension=0, tiled=True)
    own_first = first[lax.axis_index("seg")]
    dense = jnp.zeros((chan_devices, OFFBINS, LAGS), jnp.float32)
    dense = lax.dynamic_update_slice(dense, part.reshape(depth, OFFBINS, LAGS), (own_first, 0, 0))
    pieces = lax.all_to_all(dense, "chan", 0, 0, tiled=True)
    return jnp.sum(pieces, axis=0, keepdims=True)


def solution(mesh):
    placed = (P("chan", "seg", None), P("chan"), P("chan", None), P("chan", None))
    return jax.shard_map(
        shards,
        mesh=mesh,
        in_specs=placed,
        out_specs=P(("chan", "seg"), None, None),
        check_vma=False,
    )
```

```python
import math

import jax
import jax.numpy as jnp
from jax import lax
from jax.sharding import PartitionSpec as P

LAGS = 256
OFFBINS = 2


def normalize(traces, taper_len):
    values = traces.astype(jnp.float32)
    sample_count = values.shape[2]
    power = jnp.mean(values * values, axis=2, keepdims=True)
    times = jnp.arange(sample_count).astype(jnp.float32)
    length = taper_len.astype(jnp.float32)[:, None, None]
    window = jnp.minimum(1.0, jnp.minimum((times + 1.0) / length, (sample_count - times) / length))
    return (window * values * lax.rsqrt(power + 1e-06)).astype(jnp.bfloat16)


def hankel(normed, lag_count):
    chan_count, seg_count, sample_count = normed.shape
    turned = jnp.transpose(normed, (1, 2, 0))
    padded = jnp.pad(turned, ((0, 0), (lag_count // 2, lag_count // 2), (0, 0)))
    slices = [padded[:, lag_count - k : lag_count - k + sample_count, :] for k in range(lag_count)]
    picked = jnp.stack(slices, axis=3)
    return picked.reshape(seg_count * sample_count, chan_count * lag_count)


def shards(traces, taper_len, gather_id, offset_bin):
    chan_count = traces.shape[0]
    chan_devices = lax.axis_size("chan")
    seg_devices = lax.axis_size("seg")
    bucket_count = chan_devices * seg_devices * OFFBINS
    normed = normalize(traces, taper_len)
    kernel = hankel(normed, LAGS)
    first_row = lax.axis_index("chan") * chan_count
    own_rows = first_row + jnp.arange(chan_count, dtype=jnp.int32)[None, :]
    flat = lax.optimization_barrier(normed.reshape(chan_count, -1))
    copies = jnp.broadcast_to(flat[None], (chan_devices,) + flat.shape)
    piece = lax.all_to_all(copies, "chan", 0, 0, tiled=True).reshape(-1, flat.shape[1])
    row_count = piece.shape[0]
    product = jnp.dot(piece, kernel, preferred_element_type=jnp.float32)
    product = product.reshape(row_count * chan_count, LAGS)
    labels = jnp.transpose(gather_id * OFFBINS + offset_bin)
    partner = jnp.arange(row_count, dtype=jnp.int32)[:, None]
    labels = jnp.where(partner == own_rows, -1, labels).reshape(-1)
    gathers = chan_devices * seg_devices
    low_span = 2 * (row_count - 1)
    reach = (low_span + 5 * (chan_count - 1)) * gathers // (2 * low_span + 1) + 2
    depth = -(-(reach - 1) // seg_devices) + 1
    start = gather_id[0, 0]
    lanes = jnp.arange(seg_devices, dtype=jnp.int32)
    first = jnp.minimum((start - lanes + seg_devices - 1) // seg_devices, chan_devices - depth)
    first = jnp.maximum(first, 0)
    window = (first[:, None] + jnp.arange(depth, dtype=jnp.int32)[None, :]) * seg_devices + lanes[:, None]
    wanted = (window[:, :, None] * OFFBINS + jnp.arange(OFFBINS, dtype=jnp.int32)).reshape(-1)
    onehot = (wanted[:, None] == labels[None, :]).astype(jnp.bfloat16)
    high = lax.reduce_precision(product, exponent_bits=8, mantissa_bits=7)
    low = product - high
    split = jnp.concatenate([high, low], axis=1).astype(jnp.bfloat16)
    both = jnp.dot(onehot, split, preferred_element_type=jnp.float32)
    total = both[:, :LAGS] + both[:, LAGS:]
    scale = 1.0 / math.sqrt(traces.shape[2] * traces.shape[1] * seg_devices)
    stacked = (total * scale).reshape(seg_devices, depth, OFFBINS, LAGS)
    part = jnp.sum(lax.all_to_all(stacked, "seg", 0, 0, tiled=True), axis=0)
    own_first = first[lax.axis_index("seg")]
    dense = jnp.zeros((chan_devices, OFFBINS, LAGS), jnp.float32)
    dense = lax.dynamic_update_slice(dense, part.reshape(depth, OFFBINS, LAGS), (own_first, 0, 0))
    pieces = lax.all_to_all(dense, "chan", 0, 0, tiled=True)
    return jnp.sum(pieces, axis=0, keepdims=True)


def solution(mesh):
    placed = (P("chan", "seg", None), P("chan"), P("chan", None), P("chan", None))
    return jax.shard_map(
        shards,
        mesh=mesh,
        in_specs=placed,
        out_specs=P(("chan", "seg"), None, None),
        check_vma=False,
    )
```

```python
import math

import jax
import jax.numpy as jnp
from jax import lax
from jax.sharding import PartitionSpec as P

LAGS = 256
OFFBINS = 2


def normalize(traces, taper_len):
    values = traces.astype(jnp.float32)
    sample_count = values.shape[2]
    power = jnp.mean(values * values, axis=2, keepdims=True)
    times = jnp.arange(sample_count).astype(jnp.float32)
    length = taper_len.astype(jnp.float32)[:, None, None]
    window = jnp.minimum(1.0, jnp.minimum((times + 1.0) / length, (sample_count - times) / length))
    return (window * values * lax.rsqrt(power + 1e-06)).astype(jnp.bfloat16)


def toeplitz(normed, lag_count):
    chan_count, seg_count, sample_count = normed.shape
    flat = normed.reshape(chan_count, sample_count)
    half = lag_count // 2
    width = sample_count + lag_count
    ring = jnp.concatenate(
        [flat[:, half:], jnp.zeros((chan_count, width - sample_count), flat.dtype), flat[:, :half]], axis=1
    )
    tiled = jnp.tile(ring, (1, lag_count + 1))[:, : lag_count * (width - 1)]
    return tiled.reshape(chan_count, lag_count, width - 1)[:, :, :sample_count]


def shards(traces, taper_len, gather_id, offset_bin):
    chan_count = traces.shape[0]
    chan_devices = lax.axis_size("chan")
    seg_devices = lax.axis_size("seg")
    bucket_count = chan_devices * seg_devices * OFFBINS
    normed = normalize(traces, taper_len)
    kernel = toeplitz(normed, LAGS)
    first_row = lax.axis_index("chan") * chan_count
    own_rows = first_row + jnp.arange(chan_count, dtype=jnp.int32)[None, :]
    flat = lax.optimization_barrier(normed.reshape(chan_count, -1))
    copies = jnp.broadcast_to(flat[None], (chan_devices,) + flat.shape)
    piece = lax.all_to_all(copies, "chan", 0, 0, tiled=True).reshape(-1, flat.shape[1])
    row_count = piece.shape[0]
    product = jnp.einsum("it,jkt->ijk", piece, kernel, preferred_element_type=jnp.float32)
    product = product.reshape(row_count * chan_count, LAGS)
    labels = jnp.transpose(gather_id * OFFBINS + offset_bin)
    partner = jnp.arange(row_count, dtype=jnp.int32)[:, None]
    labels = jnp.where(partner == own_rows, -1, labels).reshape(-1)
    gathers = chan_devices * seg_devices
    low_span = 2 * (row_count - 1)
    reach = (low_span + 5 * (chan_count - 1)) * gathers // (2 * low_span + 1) + 2
    depth = -(-(reach - 1) // seg_devices) + 1
    start = gather_id[0, 0]
    lanes = jnp.arange(seg_devices, dtype=jnp.int32)
    first = jnp.minimum((start - lanes + seg_devices - 1) // seg_devices, chan_devices - depth)
    first = jnp.maximum(first, 0)
    window = (first[:, None] + jnp.arange(depth, dtype=jnp.int32)[None, :]) * seg_devices + lanes[:, None]
    wanted = (window[:, :, None] * OFFBINS + jnp.arange(OFFBINS, dtype=jnp.int32)).reshape(-1)
    onehot = (wanted[:, None] == labels[None, :]).astype(jnp.bfloat16)
    high = lax.reduce_precision(product, exponent_bits=8, mantissa_bits=7)
    low = product - high
    split = jnp.concatenate([high, low], axis=1).astype(jnp.bfloat16)
    both = jnp.dot(onehot, split, preferred_element_type=jnp.float32)
    total = both[:, :LAGS] + both[:, LAGS:]
    scale = 1.0 / math.sqrt(traces.shape[2] * traces.shape[1] * seg_devices)
    stacked = (total * scale).reshape(seg_devices, depth, OFFBINS, LAGS)
    part = jnp.sum(lax.all_to_all(stacked, "seg", 0, 0, tiled=True), axis=0)
    own_first = first[lax.axis_index("seg")]
    dense = jnp.zeros((chan_devices, OFFBINS, LAGS), jnp.float32)
    dense = lax.dynamic_update_slice(dense, part.reshape(depth, OFFBINS, LAGS), (own_first, 0, 0))
    pieces = lax.all_to_all(dense, "chan", 0, 0, tiled=True)
    return jnp.sum(pieces, axis=0, keepdims=True)


def solution(mesh):
    placed = (P("chan", "seg", None), P("chan"), P("chan", None), P("chan", None))
    return jax.shard_map(
        shards,
        mesh=mesh,
        in_specs=placed,
        out_specs=P(("chan", "seg"), None, None),
        check_vma=False,
    )
```

```python
import math

import jax
import jax.numpy as jnp
from jax import lax
from jax.sharding import PartitionSpec as P

LAGS = 256
OFFBINS = 2


def normalize(traces, taper_len):
    values = traces.astype(jnp.float32)
    sample_count = values.shape[2]
    power = jnp.mean(values * values, axis=2, keepdims=True)
    times = jnp.arange(sample_count).astype(jnp.float32)
    length = taper_len.astype(jnp.float32)[:, None, None]
    window = jnp.minimum(1.0, jnp.minimum((times + 1.0) / length, (sample_count - times) / length))
    return (window * values * lax.rsqrt(power + 1e-06)).astype(jnp.bfloat16)


def toeplitz(normed, lag_count):
    chan_count, seg_count, sample_count = normed.shape
    flat = normed.reshape(chan_count, sample_count)
    half = lag_count // 2
    width = sample_count + lag_count + 1
    ring = jnp.concatenate(
        [flat[:, half:], jnp.zeros((chan_count, width - sample_count), flat.dtype), flat[:, :half]], axis=1
    )
    tiled = jnp.tile(ring, (1, lag_count + 1))[:, : lag_count * (width - 1)]
    return tiled.reshape(chan_count, lag_count, width - 1)[:, :, :sample_count]


def shards(traces, taper_len, gather_id, offset_bin):
    chan_count = traces.shape[0]
    chan_devices = lax.axis_size("chan")
    seg_devices = lax.axis_size("seg")
    bucket_count = chan_devices * seg_devices * OFFBINS
    normed = normalize(traces, taper_len)
    kernel = toeplitz(normed, LAGS)
    first_row = lax.axis_index("chan") * chan_count
    own_rows = first_row + jnp.arange(chan_count, dtype=jnp.int32)[None, :]
    flat = lax.optimization_barrier(normed.reshape(chan_count, -1))
    copies = jnp.broadcast_to(flat[None], (chan_devices,) + flat.shape)
    piece = lax.all_to_all(copies, "chan", 0, 0, tiled=True).reshape(-1, flat.shape[1])
    row_count = piece.shape[0]
    product = jnp.einsum("it,jkt->ijk", piece, kernel, preferred_element_type=jnp.float32)
    product = product.reshape(row_count * chan_count, LAGS)
    labels = jnp.transpose(gather_id * OFFBINS + offset_bin)
    partner = jnp.arange(row_count, dtype=jnp.int32)[:, None]
    labels = jnp.where(partner == own_rows, -1, labels).reshape(-1)
    gathers = chan_devices * seg_devices
    low_span = 2 * (row_count - 1)
    reach = (low_span + 5 * (chan_count - 1)) * gathers // (2 * low_span + 1) + 2
    depth = -(-(reach - 1) // seg_devices) + 1
    start = gather_id[0, 0]
    lanes = jnp.arange(seg_devices, dtype=jnp.int32)
    first = jnp.minimum((start - lanes + seg_devices - 1) // seg_devices, chan_devices - depth)
    first = jnp.maximum(first, 0)
    window = (first[:, None] + jnp.arange(depth, dtype=jnp.int32)[None, :]) * seg_devices + lanes[:, None]
    wanted = (window[:, :, None] * OFFBINS + jnp.arange(OFFBINS, dtype=jnp.int32)).reshape(-1)
    onehot = (wanted[:, None] == labels[None, :]).astype(jnp.bfloat16)
    high = lax.reduce_precision(product, exponent_bits=8, mantissa_bits=7)
    low = product - high
    split = jnp.concatenate([high, low], axis=1).astype(jnp.bfloat16)
    both = jnp.dot(onehot, split, preferred_element_type=jnp.float32)
    total = both[:, :LAGS] + both[:, LAGS:]
    scale = 1.0 / math.sqrt(traces.shape[2] * traces.shape[1] * seg_devices)
    stacked = (total * scale).reshape(seg_devices, depth, OFFBINS, LAGS)
    part = jnp.sum(lax.all_to_all(stacked, "seg", 0, 0, tiled=True), axis=0)
    own_first = first[lax.axis_index("seg")]
    dense = jnp.zeros((chan_devices, OFFBINS, LAGS), jnp.float32)
    dense = lax.dynamic_update_slice(dense, part.reshape(depth, OFFBINS, LAGS), (own_first, 0, 0))
    pieces = lax.all_to_all(dense, "chan", 0, 0, tiled=True)
    return jnp.sum(pieces, axis=0, keepdims=True)


def solution(mesh):
    placed = (P("chan", "seg", None), P("chan"), P("chan", None), P("chan", None))
    return jax.shard_map(
        shards,
        mesh=mesh,
        in_specs=placed,
        out_specs=P(("chan", "seg"), None, None),
        check_vma=False,
    )
```

```python
import math

import jax
import jax.numpy as jnp
from jax import lax
from jax.sharding import PartitionSpec as P

LAGS = 256
OFFBINS = 2


def normalize(traces, taper_len):
    values = traces.astype(jnp.float32)
    sample_count = values.shape[2]
    power = jnp.mean(values * values, axis=2, keepdims=True)
    times = jnp.arange(sample_count).astype(jnp.float32)
    length = taper_len.astype(jnp.float32)[:, None, None]
    window = jnp.minimum(1.0, jnp.minimum((times + 1.0) / length, (sample_count - times) / length))
    return (window * values * lax.rsqrt(power + 1e-06)).astype(jnp.bfloat16)


def toeplitz(normed, lag_count):
    chan_count, seg_count, sample_count = normed.shape
    flat = normed.reshape(chan_count, sample_count)
    half = lag_count // 2
    width = sample_count + lag_count + 1
    ring = jnp.concatenate(
        [flat[:, half:], jnp.zeros((chan_count, width - sample_count), flat.dtype), flat[:, :half]], axis=1
    )
    tiled = jnp.tile(ring, (1, lag_count + 1))[:, : lag_count * (width - 1)]
    return tiled.reshape(chan_count, lag_count, width - 1)[:, :, :sample_count]


def shards(traces, taper_len, gather_id, offset_bin):
    chan_count = traces.shape[0]
    chan_devices = lax.axis_size("chan")
    seg_devices = lax.axis_size("seg")
    bucket_count = chan_devices * seg_devices * OFFBINS
    normed = normalize(traces, taper_len)
    kernel = toeplitz(normed, LAGS)
    first_row = lax.axis_index("chan") * chan_count
    own_rows = first_row + jnp.arange(chan_count, dtype=jnp.int32)[None, :]
    flat = lax.optimization_barrier(normed.reshape(chan_count, -1))
    copies = jnp.broadcast_to(flat[None], (chan_devices,) + flat.shape)
    piece = lax.all_to_all(copies, "chan", 0, 0, tiled=True).reshape(-1, flat.shape[1])
    row_count = piece.shape[0]
    product = jnp.einsum("it,jkt->ijk", piece, kernel, preferred_element_type=jnp.float32)
    product = jnp.transpose(product, (1, 0, 2)).reshape(row_count * chan_count, LAGS)
    labels = gather_id * OFFBINS + offset_bin
    partner = jnp.arange(row_count, dtype=jnp.int32)[None, :]
    labels = jnp.where(partner == own_rows.reshape(-1, 1), -1, labels).reshape(-1)
    gathers = chan_devices * seg_devices
    low_span = 2 * (row_count - 1)
    reach = (low_span + 5 * (chan_count - 1)) * gathers // (2 * low_span + 1) + 2
    depth = -(-(reach - 1) // seg_devices) + 1
    start = gather_id[0, 0]
    lanes = jnp.arange(seg_devices, dtype=jnp.int32)
    first = jnp.minimum((start - lanes + seg_devices - 1) // seg_devices, chan_devices - depth)
    first = jnp.maximum(first, 0)
    window = (first[:, None] + jnp.arange(depth, dtype=jnp.int32)[None, :]) * seg_devices + lanes[:, None]
    wanted = (window[:, :, None] * OFFBINS + jnp.arange(OFFBINS, dtype=jnp.int32)).reshape(-1)
    onehot = (wanted[:, None] == labels[None, :]).astype(jnp.bfloat16)
    high = lax.reduce_precision(product, exponent_bits=8, mantissa_bits=7)
    low = product - high
    split = jnp.concatenate([high, low], axis=1).astype(jnp.bfloat16)
    both = jnp.dot(onehot, split, preferred_element_type=jnp.float32)
    total = both[:, :LAGS] + both[:, LAGS:]
    scale = 1.0 / math.sqrt(traces.shape[2] * traces.shape[1] * seg_devices)
    stacked = (total * scale).reshape(seg_devices, depth, OFFBINS, LAGS)
    part = jnp.sum(lax.all_to_all(stacked, "seg", 0, 0, tiled=True), axis=0)
    own_first = first[lax.axis_index("seg")]
    dense = jnp.zeros((chan_devices, OFFBINS, LAGS), jnp.float32)
    dense = lax.dynamic_update_slice(dense, part.reshape(depth, OFFBINS, LAGS), (own_first, 0, 0))
    pieces = lax.all_to_all(dense, "chan", 0, 0, tiled=True)
    return jnp.sum(pieces, axis=0, keepdims=True)


def solution(mesh):
    placed = (P("chan", "seg", None), P("chan"), P("chan", None), P("chan", None))
    return jax.shard_map(
        shards,
        mesh=mesh,
        in_specs=placed,
        out_specs=P(("chan", "seg"), None, None),
        check_vma=False,
    )
```

```python
import math

import jax
import jax.numpy as jnp
from jax import lax
from jax.experimental import pallas as pl
from jax.experimental.pallas import tpu as pltpu
from jax.sharding import PartitionSpec as P

LAGS = 256
OFFBINS = 2


def normalize(traces, taper_len):
    values = traces.astype(jnp.float32)
    sample_count = values.shape[2]
    power = jnp.mean(values * values, axis=2, keepdims=True)
    times = jnp.arange(sample_count).astype(jnp.float32)
    length = taper_len.astype(jnp.float32)[:, None, None]
    window = jnp.minimum(1.0, jnp.minimum((times + 1.0) / length, (sample_count - times) / length))
    return (window * values * lax.rsqrt(power + 1e-06)).astype(jnp.bfloat16)


def toeplitz(normed, lag_count):
    chan_count, seg_count, sample_count = normed.shape
    flat = normed.reshape(chan_count, sample_count)
    half = lag_count // 2
    width = sample_count + lag_count + 1
    ring = jnp.concatenate(
        [flat[:, half:], jnp.zeros((chan_count, width - sample_count), flat.dtype), flat[:, :half]], axis=1
    )
    tiled = jnp.tile(ring, (1, lag_count + 1))[:, : lag_count * (width - 1)]
    return tiled.reshape(chan_count, lag_count, width - 1)[:, :, :sample_count]


def bucket_body(x_ref, t_ref, lab_ref, want_ref, o_ref):
    @pl.when(pl.program_id(0) == 0)
    def _():
        o_ref[...] = jnp.zeros_like(o_ref)

    pairs = lax.dot_general(
        x_ref[...], t_ref[0], (((1,), (1,)), ((), ())), preferred_element_type=jnp.float32
    )
    high = pairs.astype(jnp.bfloat16)
    low = (pairs - high.astype(jnp.float32)).astype(jnp.bfloat16)
    hits = jnp.where(want_ref[...] == lab_ref[0], 1.0, 0.0).astype(jnp.bfloat16)
    o_ref[...] += jnp.dot(hits, high, preferred_element_type=jnp.float32) + jnp.dot(
        hits, low, preferred_element_type=jnp.float32
    )


def bucket_sums(piece, kernel, labels, wanted):
    row_count, sample_count = piece.shape
    chan_count, lag_count, _ = kernel.shape
    rows = wanted.shape[0]
    flops = 2 * chan_count * row_count * lag_count * (sample_count + 2 * rows)
    return pl.pallas_call(
        bucket_body,
        grid=(chan_count,),
        in_specs=[
            pl.BlockSpec((row_count, sample_count), lambda j: (0, 0)),
            pl.BlockSpec((1, lag_count, sample_count), lambda j: (j, 0, 0)),
            pl.BlockSpec((1, 1, row_count), lambda j: (j, 0, 0)),
            pl.BlockSpec((rows, 1), lambda j: (0, 0)),
        ],
        out_specs=pl.BlockSpec((rows, lag_count), lambda j: (0, 0)),
        out_shape=jax.ShapeDtypeStruct((rows, lag_count), jnp.float32),
        cost_estimate=pl.CostEstimate(flops=flops, transcendentals=0, bytes_accessed=4 * rows * lag_count),
    )(piece, kernel, labels.reshape(chan_count, 1, row_count), wanted.reshape(rows, 1))


def shards(traces, taper_len, gather_id, offset_bin):
    chan_count = traces.shape[0]
    chan_devices = lax.axis_size("chan")
    seg_devices = lax.axis_size("seg")
    bucket_count = chan_devices * seg_devices * OFFBINS
    normed = normalize(traces, taper_len)
    kernel = toeplitz(normed, LAGS)
    first_row = lax.axis_index("chan") * chan_count
    own_rows = first_row + jnp.arange(chan_count, dtype=jnp.int32)[None, :]
    flat = lax.optimization_barrier(normed.reshape(chan_count, -1))
    copies = jnp.broadcast_to(flat[None], (chan_devices,) + flat.shape)
    piece = lax.all_to_all(copies, "chan", 0, 0, tiled=True).reshape(-1, flat.shape[1])
    row_count = piece.shape[0]
    labels = gather_id * OFFBINS + offset_bin
    partner = jnp.arange(row_count, dtype=jnp.int32)[None, :]
    labels = jnp.where(partner == own_rows.reshape(-1, 1), -1, labels)
    gathers = chan_devices * seg_devices
    low_span = 2 * (row_count - 1)
    reach = (low_span + 5 * (chan_count - 1)) * gathers // (2 * low_span + 1) + 2
    depth = -(-(reach - 1) // seg_devices) + 1
    start = gather_id[0, 0]
    lanes = jnp.arange(seg_devices, dtype=jnp.int32)
    first = jnp.minimum((start - lanes + seg_devices - 1) // seg_devices, chan_devices - depth)
    first = jnp.maximum(first, 0)
    window = (first[:, None] + jnp.arange(depth, dtype=jnp.int32)[None, :]) * seg_devices + lanes[:, None]
    wanted = (window[:, :, None] * OFFBINS + jnp.arange(OFFBINS, dtype=jnp.int32)).reshape(-1)
    total = bucket_sums(piece, kernel, labels, wanted)
    scale = 1.0 / math.sqrt(traces.shape[2] * traces.shape[1] * seg_devices)
    stacked = (total * scale).reshape(seg_devices, depth, OFFBINS, LAGS)
    part = jnp.sum(lax.all_to_all(stacked, "seg", 0, 0, tiled=True), axis=0)
    own_first = first[lax.axis_index("seg")]
    dense = jnp.zeros((chan_devices, OFFBINS, LAGS), jnp.float32)
    dense = lax.dynamic_update_slice(dense, part.reshape(depth, OFFBINS, LAGS), (own_first, 0, 0))
    pieces = lax.all_to_all(dense, "chan", 0, 0, tiled=True)
    return jnp.sum(pieces, axis=0, keepdims=True)


def solution(mesh):
    placed = (P("chan", "seg", None), P("chan"), P("chan", None), P("chan", None))
    return jax.shard_map(
        shards,
        mesh=mesh,
        in_specs=placed,
        out_specs=P(("chan", "seg"), None, None),
        check_vma=False,
    )
```

```python
import math

import jax
import jax.numpy as jnp
from jax import lax
from jax.experimental import pallas as pl
from jax.experimental.pallas import tpu as pltpu
from jax.sharding import PartitionSpec as P

LAGS = 256
OFFBINS = 2


def normalize(traces, taper_len):
    values = traces.astype(jnp.float32)
    sample_count = values.shape[2]
    power = jnp.mean(values * values, axis=2, keepdims=True)
    times = jnp.arange(sample_count).astype(jnp.float32)
    length = taper_len.astype(jnp.float32)[:, None, None]
    window = jnp.minimum(1.0, jnp.minimum((times + 1.0) / length, (sample_count - times) / length))
    return (window * values * lax.rsqrt(power + 1e-06)).astype(jnp.bfloat16)


def toeplitz(normed, lag_count):
    chan_count, seg_count, sample_count = normed.shape
    flat = normed.reshape(chan_count, sample_count)
    half = lag_count // 2
    width = sample_count + lag_count + 1
    ring = jnp.concatenate(
        [flat[:, half:], jnp.zeros((chan_count, width - sample_count), flat.dtype), flat[:, :half]], axis=1
    )
    tiled = jnp.tile(ring, (1, lag_count + 1))[:, : lag_count * (width - 1)]
    return tiled.reshape(chan_count, lag_count, width - 1)[:, :, :sample_count]


def bucket_body(x_ref, t_ref, lab_ref, o_ref):
    @pl.when(pl.program_id(0) == 0)
    def _():
        o_ref[...] = jnp.zeros_like(o_ref)

    pairs = lax.dot_general(
        x_ref[...], t_ref[0], (((1,), (1,)), ((), ())), preferred_element_type=jnp.float32
    )
    high = pairs.astype(jnp.bfloat16)
    low = (pairs - high.astype(jnp.float32)).astype(jnp.bfloat16)
    hits = lab_ref[0]
    o_ref[...] += jnp.dot(hits, high, preferred_element_type=jnp.float32) + jnp.dot(
        hits, low, preferred_element_type=jnp.float32
    )


def bucket_sums(piece, kernel, labels, wanted):
    row_count, sample_count = piece.shape
    chan_count, lag_count, _ = kernel.shape
    rows = wanted.shape[0]
    hits = (wanted[None, :, None] == labels[:, None, :]).astype(jnp.bfloat16)
    flops = 2 * chan_count * row_count * lag_count * (sample_count + 2 * rows)
    return pl.pallas_call(
        bucket_body,
        grid=(chan_count,),
        in_specs=[
            pl.BlockSpec((row_count, sample_count), lambda j: (0, 0)),
            pl.BlockSpec((1, lag_count, sample_count), lambda j: (j, 0, 0)),
            pl.BlockSpec((1, rows, row_count), lambda j: (j, 0, 0)),
        ],
        out_specs=pl.BlockSpec((rows, lag_count), lambda j: (0, 0)),
        out_shape=jax.ShapeDtypeStruct((rows, lag_count), jnp.float32),
        cost_estimate=pl.CostEstimate(flops=flops, transcendentals=0, bytes_accessed=4 * rows * lag_count),
    )(piece, kernel, hits)


def shards(traces, taper_len, gather_id, offset_bin):
    chan_count = traces.shape[0]
    chan_devices = lax.axis_size("chan")
    seg_devices = lax.axis_size("seg")
    bucket_count = chan_devices * seg_devices * OFFBINS
    normed = normalize(traces, taper_len)
    kernel = toeplitz(normed, LAGS)
    first_row = lax.axis_index("chan") * chan_count
    own_rows = first_row + jnp.arange(chan_count, dtype=jnp.int32)[None, :]
    flat = lax.optimization_barrier(normed.reshape(chan_count, -1))
    copies = jnp.broadcast_to(flat[None], (chan_devices,) + flat.shape)
    piece = lax.all_to_all(copies, "chan", 0, 0, tiled=True).reshape(-1, flat.shape[1])
    row_count = piece.shape[0]
    labels = gather_id * OFFBINS + offset_bin
    partner = jnp.arange(row_count, dtype=jnp.int32)[None, :]
    labels = jnp.where(partner == own_rows.reshape(-1, 1), -1, labels)
    gathers = chan_devices * seg_devices
    low_span = 2 * (row_count - 1)
    reach = (low_span + 5 * (chan_count - 1)) * gathers // (2 * low_span + 1) + 2
    depth = -(-(reach - 1) // seg_devices) + 1
    start = gather_id[0, 0]
    lanes = jnp.arange(seg_devices, dtype=jnp.int32)
    first = jnp.minimum((start - lanes + seg_devices - 1) // seg_devices, chan_devices - depth)
    first = jnp.maximum(first, 0)
    window = (first[:, None] + jnp.arange(depth, dtype=jnp.int32)[None, :]) * seg_devices + lanes[:, None]
    wanted = (window[:, :, None] * OFFBINS + jnp.arange(OFFBINS, dtype=jnp.int32)).reshape(-1)
    total = bucket_sums(piece, kernel, labels, wanted)
    scale = 1.0 / math.sqrt(traces.shape[2] * traces.shape[1] * seg_devices)
    stacked = (total * scale).reshape(seg_devices, depth, OFFBINS, LAGS)
    part = jnp.sum(lax.all_to_all(stacked, "seg", 0, 0, tiled=True), axis=0)
    own_first = first[lax.axis_index("seg")]
    dense = jnp.zeros((chan_devices, OFFBINS, LAGS), jnp.float32)
    dense = lax.dynamic_update_slice(dense, part.reshape(depth, OFFBINS, LAGS), (own_first, 0, 0))
    pieces = lax.all_to_all(dense, "chan", 0, 0, tiled=True)
    return jnp.sum(pieces, axis=0, keepdims=True)


def solution(mesh):
    placed = (P("chan", "seg", None), P("chan"), P("chan", None), P("chan", None))
    return jax.shard_map(
        shards,
        mesh=mesh,
        in_specs=placed,
        out_specs=P(("chan", "seg"), None, None),
        check_vma=False,
    )
```

```python
import math

import jax
import jax.numpy as jnp
from jax import lax
from jax.sharding import PartitionSpec as P

LAGS = 256
OFFBINS = 2


def normalize(traces, taper_len):
    values = traces.astype(jnp.float32)
    sample_count = values.shape[2]
    power = jnp.mean(values * values, axis=2, keepdims=True)
    times = jnp.arange(sample_count).astype(jnp.float32)
    length = taper_len.astype(jnp.float32)[:, None, None]
    window = jnp.minimum(1.0, jnp.minimum((times + 1.0) / length, (sample_count - times) / length))
    return (window * values * lax.rsqrt(power + 1e-06)).astype(jnp.bfloat16)


def toeplitz(normed, lag_count):
    chan_count, seg_count, sample_count = normed.shape
    flat = normed.reshape(chan_count, sample_count)
    half = lag_count // 2
    width = sample_count + lag_count + 1
    ring = jnp.concatenate(
        [flat[:, half:], jnp.zeros((chan_count, width - sample_count), flat.dtype), flat[:, :half]], axis=1
    )
    tiled = jnp.tile(ring, (1, lag_count + 1))[:, : lag_count * (width - 1)]
    return tiled.reshape(chan_count, lag_count, width - 1)[:, :, :sample_count]


def shards(traces, taper_len, gather_id, offset_bin):
    chan_count = traces.shape[0]
    chan_devices = lax.axis_size("chan")
    seg_devices = lax.axis_size("seg")
    bucket_count = chan_devices * seg_devices * OFFBINS
    normed = normalize(traces, taper_len)
    kernel = toeplitz(normed, LAGS)
    first_row = lax.axis_index("chan") * chan_count
    own_rows = first_row + jnp.arange(chan_count, dtype=jnp.int32)[None, :]
    flat = lax.optimization_barrier(normed.reshape(chan_count, -1))
    copies = jnp.broadcast_to(flat[None], (chan_devices,) + flat.shape)
    piece = lax.all_to_all(copies, "chan", 0, 0, tiled=True).reshape(-1, flat.shape[1])
    row_count = piece.shape[0]
    product = jnp.einsum("it,jkt->ijk", piece, kernel, preferred_element_type=jnp.float32)
    product = jnp.transpose(product, (1, 0, 2)).reshape(row_count * chan_count, LAGS)
    labels = gather_id * OFFBINS + offset_bin
    partner = jnp.arange(row_count, dtype=jnp.int32)[None, :]
    labels = jnp.where(partner == own_rows.reshape(-1, 1), -1, labels).reshape(-1)
    gathers = chan_devices * seg_devices
    low_span = 2 * (row_count - 1)
    reach = (low_span + 5 * (chan_count - 1)) * gathers // (2 * low_span + 1) + 2
    depth = -(-(reach - 1) // seg_devices) + 1
    start = gather_id[0, 0]
    lanes = jnp.arange(seg_devices, dtype=jnp.int32)
    first = jnp.minimum((start - lanes + seg_devices - 1) // seg_devices, chan_devices - depth)
    first = jnp.maximum(first, 0)
    window = (first[:, None] + jnp.arange(depth, dtype=jnp.int32)[None, :]) * seg_devices + lanes[:, None]
    wanted = (window[:, :, None] * OFFBINS + jnp.arange(OFFBINS, dtype=jnp.int32)).reshape(-1)
    onehot = lax.optimization_barrier((wanted[:, None] == labels[None, :]).astype(jnp.bfloat16))
    high = lax.reduce_precision(product, exponent_bits=8, mantissa_bits=7)
    low = product - high
    split = jnp.concatenate([high, low], axis=1).astype(jnp.bfloat16)
    both = jnp.dot(onehot, split, preferred_element_type=jnp.float32)
    total = both[:, :LAGS] + both[:, LAGS:]
    scale = 1.0 / math.sqrt(traces.shape[2] * traces.shape[1] * seg_devices)
    stacked = (total * scale).reshape(seg_devices, depth, OFFBINS, LAGS)
    part = jnp.sum(lax.all_to_all(stacked, "seg", 0, 0, tiled=True), axis=0)
    own_first = first[lax.axis_index("seg")]
    dense = jnp.zeros((chan_devices, OFFBINS, LAGS), jnp.float32)
    dense = lax.dynamic_update_slice(dense, part.reshape(depth, OFFBINS, LAGS), (own_first, 0, 0))
    pieces = lax.all_to_all(dense, "chan", 0, 0, tiled=True)
    return jnp.sum(pieces, axis=0, keepdims=True)


def solution(mesh):
    placed = (P("chan", "seg", None), P("chan"), P("chan", None), P("chan", None))
    return jax.shard_map(
        shards,
        mesh=mesh,
        in_specs=placed,
        out_specs=P(("chan", "seg"), None, None),
        check_vma=False,
    )
```

```python
import math

import jax
import jax.numpy as jnp
from jax import lax
from jax.sharding import PartitionSpec as P

LAGS = 256
OFFBINS = 2


def normalize(traces, taper_len):
    values = traces.astype(jnp.float32)
    sample_count = values.shape[2]
    power = jnp.mean(values * values, axis=2, keepdims=True)
    times = jnp.arange(sample_count).astype(jnp.float32)
    length = taper_len.astype(jnp.float32)[:, None, None]
    window = jnp.minimum(1.0, jnp.minimum((times + 1.0) / length, (sample_count - times) / length))
    return (window * values * lax.rsqrt(power + 1e-06)).astype(jnp.bfloat16)


def toeplitz(normed, lag_count):
    chan_count, seg_count, sample_count = normed.shape
    flat = normed.reshape(chan_count, sample_count)
    half = lag_count // 2
    width = sample_count + lag_count + 1
    ring = jnp.concatenate(
        [flat[:, half:], jnp.zeros((chan_count, width - sample_count), flat.dtype), flat[:, :half]], axis=1
    )
    tiled = jnp.tile(ring, (1, lag_count + 1))[:, : lag_count * (width - 1)]
    return tiled.reshape(chan_count, lag_count, width - 1)[:, :, :sample_count]


def shards(traces, taper_len, gather_id, offset_bin):
    chan_count = traces.shape[0]
    chan_devices = lax.axis_size("chan")
    seg_devices = lax.axis_size("seg")
    bucket_count = chan_devices * seg_devices * OFFBINS
    normed = normalize(traces, taper_len)
    kernel = toeplitz(normed, LAGS)
    first_row = lax.axis_index("chan") * chan_count
    own_rows = first_row + jnp.arange(chan_count, dtype=jnp.int32)[None, :]
    flat = lax.optimization_barrier(normed.reshape(chan_count, -1))
    copies = jnp.broadcast_to(flat[None], (chan_devices,) + flat.shape)
    piece = lax.all_to_all(copies, "chan", 0, 0, tiled=True).reshape(-1, flat.shape[1])
    row_count = piece.shape[0]
    product = jnp.einsum("it,jkt->ijk", piece, kernel, preferred_element_type=jnp.float32)
    product = jnp.transpose(product, (1, 0, 2)).reshape(row_count * chan_count, LAGS)
    labels = gather_id * OFFBINS + offset_bin
    partner = jnp.arange(row_count, dtype=jnp.int32)[None, :]
    labels = jnp.where(partner == own_rows.reshape(-1, 1), -1, labels).reshape(-1)
    gathers = chan_devices * seg_devices
    low_span = 2 * (row_count - 1)
    reach = (low_span + 5 * (chan_count - 1)) * gathers // (2 * low_span + 1) + 2
    depth = -(-(reach - 1) // seg_devices) + 1
    start = gather_id[0, 0]
    lanes = jnp.arange(seg_devices, dtype=jnp.int32)
    first = jnp.minimum((start - lanes + seg_devices - 1) // seg_devices, chan_devices - depth)
    first = jnp.maximum(first, 0)
    window = (first[:, None] + jnp.arange(depth, dtype=jnp.int32)[None, :]) * seg_devices + lanes[:, None]
    wanted = (window[:, :, None] * OFFBINS + jnp.arange(OFFBINS, dtype=jnp.int32)).reshape(-1)
    onehot = (wanted[:, None] == labels[None, :]).astype(jnp.bfloat16)
    high = lax.reduce_precision(product, exponent_bits=8, mantissa_bits=7)
    low = product - high
    split = jnp.concatenate([high, low], axis=1).astype(jnp.bfloat16)
    both = jnp.dot(onehot, split, preferred_element_type=jnp.float32)
    total = both[:, :LAGS] + both[:, LAGS:]
    scale = 1.0 / math.sqrt(traces.shape[2] * traces.shape[1] * seg_devices)
    stacked = (total * scale).reshape(seg_devices, depth, OFFBINS, LAGS)
    part = jnp.sum(lax.all_to_all(stacked, "seg", 0, 0, tiled=True), axis=0)
    own_first = first[lax.axis_index("seg")]
    dense = jnp.zeros((chan_devices, OFFBINS, LAGS), jnp.float32)
    dense = lax.dynamic_update_slice(dense, part.reshape(depth, OFFBINS, LAGS), (own_first, 0, 0))
    me = lax.axis_index("chan")
    reach_bit = chan_devices // 2
    while reach_bit >= 1:
        halves = dense.reshape(2, -1, OFFBINS, LAGS)
        mine = (me // reach_bit) % 2
        keep = jnp.where(mine == 0, halves[0], halves[1])
        give = jnp.where(mine == 0, halves[1], halves[0])
        pairs = [(c, c ^ reach_bit) for c in range(chan_devices)]
        dense = keep + lax.ppermute(give, "chan", pairs)
        reach_bit //= 2
    return dense


def solution(mesh):
    placed = (P("chan", "seg", None), P("chan"), P("chan", None), P("chan", None))
    return jax.shard_map(
        shards,
        mesh=mesh,
        in_specs=placed,
        out_specs=P(("chan", "seg"), None, None),
        check_vma=False,
    )
```

```python
import math

import jax
import jax.numpy as jnp
from jax import lax
from jax.sharding import PartitionSpec as P

LAGS = 256
OFFBINS = 2


def normalize(traces, taper_len):
    values = traces.astype(jnp.float32)
    sample_count = values.shape[2]
    power = jnp.mean(values * values, axis=2, keepdims=True)
    times = jnp.arange(sample_count).astype(jnp.float32)
    length = taper_len.astype(jnp.float32)[:, None, None]
    window = jnp.minimum(1.0, jnp.minimum((times + 1.0) / length, (sample_count - times) / length))
    return (window * values * lax.rsqrt(power + 1e-06)).astype(jnp.bfloat16)


def toeplitz(normed, lag_count):
    chan_count, seg_count, sample_count = normed.shape
    flat = normed.reshape(chan_count, sample_count)
    half = lag_count // 2
    width = sample_count + lag_count + 1
    ring = jnp.concatenate(
        [flat[:, half:], jnp.zeros((chan_count, width - sample_count), flat.dtype), flat[:, :half]], axis=1
    )
    tiled = jnp.tile(ring, (1, lag_count + 1))[:, : lag_count * (width - 1)]
    return tiled.reshape(chan_count, lag_count, width - 1)[:, :, :sample_count]


def shards(traces, taper_len, gather_id, offset_bin):
    chan_count = traces.shape[0]
    chan_devices = lax.axis_size("chan")
    seg_devices = lax.axis_size("seg")
    bucket_count = chan_devices * seg_devices * OFFBINS
    normed = normalize(traces, taper_len)
    kernel = toeplitz(normed, LAGS)
    first_row = lax.axis_index("chan") * chan_count
    own_rows = first_row + jnp.arange(chan_count, dtype=jnp.int32)[None, :]
    flat = lax.optimization_barrier(normed.reshape(chan_count, -1))
    copies = jnp.broadcast_to(flat[None], (chan_devices,) + flat.shape)
    piece = lax.all_to_all(copies, "chan", 0, 0, tiled=True).reshape(-1, flat.shape[1])
    row_count = piece.shape[0]
    product = jnp.einsum("it,jkt->ijk", piece, kernel, preferred_element_type=jnp.float32)
    product = jnp.transpose(product, (1, 0, 2)).reshape(row_count * chan_count, LAGS)
    labels = gather_id * OFFBINS + offset_bin
    partner = jnp.arange(row_count, dtype=jnp.int32)[None, :]
    labels = jnp.where(partner == own_rows.reshape(-1, 1), -1, labels).reshape(-1)
    gathers = chan_devices * seg_devices
    low_span = 2 * (row_count - 1)
    reach = (low_span + 5 * (chan_count - 1)) * gathers // (2 * low_span + 1) + 2
    depth = -(-(reach - 1) // seg_devices) + 1
    depth = -(-depth * OFFBINS // 8) * 8 // OFFBINS
    start = gather_id[0, 0]
    lanes = jnp.arange(seg_devices, dtype=jnp.int32)
    first = jnp.minimum((start - lanes + seg_devices - 1) // seg_devices, chan_devices - depth)
    first = jnp.maximum(first, 0)
    window = (first[:, None] + jnp.arange(depth, dtype=jnp.int32)[None, :]) * seg_devices + lanes[:, None]
    wanted = (window[:, :, None] * OFFBINS + jnp.arange(OFFBINS, dtype=jnp.int32)).reshape(-1)
    onehot = (wanted[:, None] == labels[None, :]).astype(jnp.bfloat16)
    high = lax.reduce_precision(product, exponent_bits=8, mantissa_bits=7)
    low = product - high
    split = jnp.concatenate([high, low], axis=1).astype(jnp.bfloat16)
    both = jnp.dot(onehot, split, preferred_element_type=jnp.float32)
    total = both[:, :LAGS] + both[:, LAGS:]
    scale = 1.0 / math.sqrt(traces.shape[2] * traces.shape[1] * seg_devices)
    stacked = (total * scale).reshape(seg_devices, depth * OFFBINS, LAGS)
    part = jnp.sum(lax.all_to_all(stacked, "seg", 0, 0, tiled=True), axis=0)
    own_first = first[lax.axis_index("seg")]
    dense = jnp.zeros((chan_devices, OFFBINS, LAGS), jnp.float32)
    dense = lax.dynamic_update_slice(dense, part.reshape(depth, OFFBINS, LAGS), (own_first, 0, 0))
    pieces = lax.all_to_all(dense, "chan", 0, 0, tiled=True)
    return jnp.sum(pieces, axis=0, keepdims=True)


def solution(mesh):
    placed = (P("chan", "seg", None), P("chan"), P("chan", None), P("chan", None))
    return jax.shard_map(
        shards,
        mesh=mesh,
        in_specs=placed,
        out_specs=P(("chan", "seg"), None, None),
        check_vma=False,
    )
```

```python
import math

import jax
import jax.numpy as jnp
from jax import lax
from jax.sharding import PartitionSpec as P

LAGS = 256
OFFBINS = 2


def normalize(traces, taper_len):
    values = traces.astype(jnp.float32)
    sample_count = values.shape[2]
    power = jnp.mean(values * values, axis=2, keepdims=True)
    times = jnp.arange(sample_count).astype(jnp.float32)
    length = taper_len.astype(jnp.float32)[:, None, None]
    window = jnp.minimum(1.0, jnp.minimum((times + 1.0) / length, (sample_count - times) / length))
    return (window * values * lax.rsqrt(power + 1e-06)).astype(jnp.bfloat16)


def toeplitz(normed, lag_count):
    chan_count, seg_count, sample_count = normed.shape
    flat = normed.reshape(chan_count, sample_count)
    half = lag_count // 2
    width = sample_count + lag_count + 1
    ring = jnp.concatenate(
        [flat[:, half:], jnp.zeros((chan_count, width - sample_count), flat.dtype), flat[:, :half]], axis=1
    )
    tiled = jnp.tile(ring, (1, lag_count + 1))[:, : lag_count * (width - 1)]
    return tiled.reshape(chan_count, lag_count, width - 1)[:, :, :sample_count]


def shards(traces, taper_len, gather_id, offset_bin):
    chan_count = traces.shape[0]
    chan_devices = lax.axis_size("chan")
    seg_devices = lax.axis_size("seg")
    bucket_count = chan_devices * seg_devices * OFFBINS
    normed = normalize(traces, taper_len)
    kernel = toeplitz(normed, LAGS)
    first_row = lax.axis_index("chan") * chan_count
    own_rows = first_row + jnp.arange(chan_count, dtype=jnp.int32)[None, :]
    flat = lax.optimization_barrier(normed.reshape(chan_count, -1))
    copies = jnp.broadcast_to(flat[None], (chan_devices,) + flat.shape)
    piece = lax.all_to_all(copies, "chan", 0, 0, tiled=True).reshape(-1, flat.shape[1])
    row_count = piece.shape[0]
    sample_count = piece.shape[1]
    me = lax.axis_index("chan")
    half = chan_devices // 2
    take = (half + 1) * chan_count
    near = lax.dynamic_slice(jnp.concatenate([piece, piece], axis=0), (me * chan_count, 0), (take, sample_count))
    block_of = jnp.arange(half + 1, dtype=jnp.int32)
    weight = jnp.where(block_of == 0, 0.5, 1.0)
    weight = jnp.where((block_of == half) & (me >= half), 0.0, weight)
    weight = jnp.repeat(weight, chan_count)
    product = jnp.einsum("it,jkt->ijk", near, kernel, preferred_element_type=jnp.float32)
    product = jnp.transpose(product, (1, 0, 2)).reshape(take * chan_count, LAGS)
    late = jnp.concatenate([jnp.zeros((chan_count, LAGS // 2), flat.dtype), flat[:, : sample_count - LAGS // 2]], axis=1)
    edge = jnp.einsum("it,jt->ji", near, late, preferred_element_type=jnp.float32).reshape(-1, 1)
    labels = gather_id * OFFBINS + offset_bin
    labels = lax.dynamic_slice(jnp.concatenate([labels, labels], axis=1), (0, me * chan_count), (chan_count, take))
    partner = jnp.arange(take, dtype=jnp.int32)[None, :]
    labels = jnp.where(partner == jnp.arange(chan_count, dtype=jnp.int32)[:, None], -1, labels).reshape(-1)
    gathers = chan_devices * seg_devices
    low_span = 2 * (row_count - 1)
    reach = (low_span + 5 * (chan_count - 1)) * gathers // (2 * low_span + 1) + 2
    depth = -(-(reach - 1) // seg_devices) + 1
    start = gather_id[0, 0]
    lanes = jnp.arange(seg_devices, dtype=jnp.int32)
    first = jnp.minimum((start - lanes + seg_devices - 1) // seg_devices, chan_devices - depth)
    first = jnp.maximum(first, 0)
    window = (first[:, None] + jnp.arange(depth, dtype=jnp.int32)[None, :]) * seg_devices + lanes[:, None]
    wanted = (window[:, :, None] * OFFBINS + jnp.arange(OFFBINS, dtype=jnp.int32)).reshape(-1)
    hit = wanted[:, None] == labels[None, :]
    onehot = jnp.where(hit, jnp.tile(weight, chan_count)[None, :], 0.0).astype(jnp.bfloat16)
    extended = jnp.concatenate([product, edge], axis=1)
    high = lax.reduce_precision(extended, exponent_bits=8, mantissa_bits=7)
    low = extended - high
    split = jnp.concatenate([high[:, :LAGS], low[:, :LAGS]], axis=1).astype(jnp.bfloat16)
    both = jnp.dot(onehot, split, preferred_element_type=jnp.float32)
    ends = jnp.concatenate([high[:, LAGS:], low[:, LAGS:]], axis=1).astype(jnp.bfloat16)
    tail = jnp.dot(onehot, ends, preferred_element_type=jnp.float32)
    direct = both[:, :LAGS] + both[:, LAGS:]
    mirror = jnp.concatenate([tail[:, :1] + tail[:, 1:], jnp.flip(direct[:, 1:], axis=1)], axis=1)
    total = direct + mirror
    scale = 1.0 / math.sqrt(traces.shape[2] * traces.shape[1] * seg_devices)
    stacked = (total * scale).reshape(seg_devices, depth, OFFBINS, LAGS)
    part = jnp.sum(lax.all_to_all(stacked, "seg", 0, 0, tiled=True), axis=0)
    own_first = first[lax.axis_index("seg")]
    dense = jnp.zeros((chan_devices, OFFBINS, LAGS), jnp.float32)
    dense = lax.dynamic_update_slice(dense, part.reshape(depth, OFFBINS, LAGS), (own_first, 0, 0))
    pieces = lax.all_to_all(dense, "chan", 0, 0, tiled=True)
    return jnp.sum(pieces, axis=0, keepdims=True)


def solution(mesh):
    placed = (P("chan", "seg", None), P("chan"), P("chan", None), P("chan", None))
    return jax.shard_map(
        shards,
        mesh=mesh,
        in_specs=placed,
        out_specs=P(("chan", "seg"), None, None),
        check_vma=False,
    )
```

```python
import math

import jax
import jax.numpy as jnp
from jax import lax
from jax.sharding import PartitionSpec as P

LAGS = 256
OFFBINS = 2


def normalize(traces, taper_len):
    values = traces.astype(jnp.float32)
    sample_count = values.shape[2]
    power = jnp.mean(values * values, axis=2, keepdims=True)
    times = jnp.arange(sample_count).astype(jnp.float32)
    length = taper_len.astype(jnp.float32)[:, None, None]
    window = jnp.minimum(1.0, jnp.minimum((times + 1.0) / length, (sample_count - times) / length))
    return (window * values * lax.rsqrt(power + 1e-06)).astype(jnp.bfloat16)


def toeplitz(normed, lag_count):
    chan_count, seg_count, sample_count = normed.shape
    flat = normed.reshape(chan_count, sample_count)
    half = lag_count // 2
    width = sample_count + lag_count + 1
    ring = jnp.concatenate(
        [flat[:, half:], jnp.zeros((chan_count, width - sample_count), flat.dtype), flat[:, :half]], axis=1
    )
    tiled = jnp.tile(ring, (1, lag_count + 1))[:, : lag_count * (width - 1)]
    return tiled.reshape(chan_count, lag_count, width - 1)[:, :, :sample_count]


def shards(traces, taper_len, gather_id, offset_bin):
    chan_count = traces.shape[0]
    chan_devices = lax.axis_size("chan")
    seg_devices = lax.axis_size("seg")
    bucket_count = chan_devices * seg_devices * OFFBINS
    normed = normalize(traces, taper_len)
    kernel = toeplitz(normed, LAGS)
    first_row = lax.axis_index("chan") * chan_count
    own_rows = first_row + jnp.arange(chan_count, dtype=jnp.int32)[None, :]
    flat = lax.optimization_barrier(normed.reshape(chan_count, -1))
    copies = jnp.broadcast_to(flat[None], (chan_devices,) + flat.shape)
    piece = lax.all_to_all(copies, "chan", 0, 0, tiled=True).reshape(-1, flat.shape[1])
    row_count = piece.shape[0]
    sample_count = piece.shape[1]
    me = lax.axis_index("chan")
    half = chan_devices // 2
    take = (half + 1) * chan_count
    near = lax.dynamic_slice(jnp.concatenate([piece, piece], axis=0), (me * chan_count, 0), (take, sample_count))
    block_of = jnp.arange(half + 1, dtype=jnp.int32)
    weight = jnp.where(block_of == 0, 0.5, 1.0)
    weight = jnp.where((block_of == half) & (me >= half), 0.0, weight)
    weight = jnp.repeat(weight, chan_count)
    product = jnp.einsum("it,jkt->ijk", near, kernel, preferred_element_type=jnp.float32)
    product = jnp.transpose(product, (1, 0, 2)).reshape(take * chan_count, LAGS)
    late = jnp.concatenate([jnp.zeros((chan_count, LAGS // 2), flat.dtype), flat[:, : sample_count - LAGS // 2]], axis=1)
    edge = jnp.einsum("it,jt->ji", near, late, preferred_element_type=jnp.float32).reshape(-1, 1)
    labels = gather_id * OFFBINS + offset_bin
    labels = lax.dynamic_slice(jnp.concatenate([labels, labels], axis=1), (0, me * chan_count), (chan_count, take))
    partner = jnp.arange(take, dtype=jnp.int32)[None, :]
    labels = jnp.where(partner == jnp.arange(chan_count, dtype=jnp.int32)[:, None], -1, labels).reshape(-1)
    gathers = chan_devices * seg_devices
    low_span = 2 * (row_count - 1)
    reach = (low_span + 5 * (chan_count - 1)) * gathers // (2 * low_span + 1) + 2
    depth = -(-(reach - 1) // seg_devices) + 1
    start = gather_id[0, 0]
    lanes = jnp.arange(seg_devices, dtype=jnp.int32)
    first = jnp.minimum((start - lanes + seg_devices - 1) // seg_devices, chan_devices - depth)
    first = jnp.maximum(first, 0)
    window = (first[:, None] + jnp.arange(depth, dtype=jnp.int32)[None, :]) * seg_devices + lanes[:, None]
    wanted = (window[:, :, None] * OFFBINS + jnp.arange(OFFBINS, dtype=jnp.int32)).reshape(-1)
    hit = wanted[:, None] == labels[None, :]
    onehot = jnp.where(hit, jnp.tile(weight, chan_count)[None, :], 0.0).astype(jnp.bfloat16)
    high = lax.reduce_precision(product, exponent_bits=8, mantissa_bits=7)
    low = product - high
    split = jnp.concatenate([high, low], axis=1).astype(jnp.bfloat16)
    both = jnp.dot(onehot, split, preferred_element_type=jnp.float32)
    edge_high = lax.reduce_precision(edge, exponent_bits=8, mantissa_bits=7)
    ends = jnp.concatenate([edge_high, edge - edge_high], axis=1).astype(jnp.bfloat16)
    tail = jnp.dot(onehot, ends, preferred_element_type=jnp.float32)
    direct = both[:, :LAGS] + both[:, LAGS:]
    mirror = jnp.concatenate([tail[:, :1] + tail[:, 1:], jnp.flip(direct[:, 1:], axis=1)], axis=1)
    total = direct + mirror
    scale = 1.0 / math.sqrt(traces.shape[2] * traces.shape[1] * seg_devices)
    stacked = (total * scale).reshape(seg_devices, depth, OFFBINS, LAGS)
    part = jnp.sum(lax.all_to_all(stacked, "seg", 0, 0, tiled=True), axis=0)
    own_first = first[lax.axis_index("seg")]
    dense = jnp.zeros((chan_devices, OFFBINS, LAGS), jnp.float32)
    dense = lax.dynamic_update_slice(dense, part.reshape(depth, OFFBINS, LAGS), (own_first, 0, 0))
    pieces = lax.all_to_all(dense, "chan", 0, 0, tiled=True)
    return jnp.sum(pieces, axis=0, keepdims=True)


def solution(mesh):
    placed = (P("chan", "seg", None), P("chan"), P("chan", None), P("chan", None))
    return jax.shard_map(
        shards,
        mesh=mesh,
        in_specs=placed,
        out_specs=P(("chan", "seg"), None, None),
        check_vma=False,
    )
```

```python
import math

import jax
import jax.numpy as jnp
from jax import lax
from jax.sharding import PartitionSpec as P

LAGS = 256
OFFBINS = 2


def normalize(traces, taper_len):
    values = traces.astype(jnp.float32)
    sample_count = values.shape[2]
    power = jnp.mean(values * values, axis=2, keepdims=True)
    times = jnp.arange(sample_count).astype(jnp.float32)
    length = taper_len.astype(jnp.float32)[:, None, None]
    window = jnp.minimum(1.0, jnp.minimum((times + 1.0) / length, (sample_count - times) / length))
    return (window * values * lax.rsqrt(power + 1e-06)).astype(jnp.bfloat16)


def toeplitz(normed, lag_count):
    chan_count, seg_count, sample_count = normed.shape
    flat = normed.reshape(chan_count, sample_count)
    half = lag_count // 2
    width = sample_count + lag_count + 1
    ring = jnp.concatenate(
        [flat[:, half:], jnp.zeros((chan_count, width - sample_count), flat.dtype), flat[:, :half]], axis=1
    )
    tiled = jnp.tile(ring, (1, lag_count + 1))[:, : lag_count * (width - 1)]
    return tiled.reshape(chan_count, lag_count, width - 1)[:, :, :sample_count]


def shards(traces, taper_len, gather_id, offset_bin):
    chan_count = traces.shape[0]
    chan_devices = lax.axis_size("chan")
    seg_devices = lax.axis_size("seg")
    bucket_count = chan_devices * seg_devices * OFFBINS
    normed = normalize(traces, taper_len)
    kernel = toeplitz(normed, LAGS)
    first_row = lax.axis_index("chan") * chan_count
    own_rows = first_row + jnp.arange(chan_count, dtype=jnp.int32)[None, :]
    flat = lax.optimization_barrier(normed.reshape(chan_count, -1))
    copies = jnp.broadcast_to(flat[None], (chan_devices,) + flat.shape)
    piece = lax.all_to_all(copies, "chan", 0, 0, tiled=True).reshape(-1, flat.shape[1])
    row_count = piece.shape[0]
    sample_count = piece.shape[1]
    me = lax.axis_index("chan")
    half = chan_devices // 2
    take = (half + 1) * chan_count
    near = lax.dynamic_slice(jnp.concatenate([piece, piece], axis=0), (me * chan_count, 0), (take, sample_count))
    block_of = jnp.arange(half + 1, dtype=jnp.int32)
    weight = jnp.where(block_of == 0, 0.5, 1.0)
    weight = jnp.where((block_of == half) & (me >= half), 0.0, weight)
    weight = jnp.repeat(weight, chan_count)
    product = jnp.einsum("it,jkt->ijk", near, kernel, preferred_element_type=jnp.float32)
    product = jnp.transpose(product, (1, 0, 2)).reshape(take * chan_count, LAGS)
    late = jnp.concatenate([jnp.zeros((chan_count, LAGS // 2), flat.dtype), flat[:, : sample_count - LAGS // 2]], axis=1)
    edge = jnp.einsum("it,jt->ji", near, late, preferred_element_type=jnp.float32).reshape(-1, 1)
    labels = gather_id * OFFBINS + offset_bin
    labels = lax.dynamic_slice(jnp.concatenate([labels, labels], axis=1), (0, me * chan_count), (chan_count, take))
    partner = jnp.arange(take, dtype=jnp.int32)[None, :]
    labels = jnp.where(partner == jnp.arange(chan_count, dtype=jnp.int32)[:, None], -1, labels).reshape(-1)
    gathers = chan_devices * seg_devices
    low_span = 2 * (row_count - 1)
    reach = (low_span + 5 * (chan_count - 1)) * gathers // (2 * low_span + 1) + 2
    depth = -(-(reach - 1) // seg_devices) + 1
    depth = -(-depth * OFFBINS // 8) * 8 // OFFBINS
    start = gather_id[0, 0]
    lanes = jnp.arange(seg_devices, dtype=jnp.int32)
    first = jnp.minimum((start - lanes + seg_devices - 1) // seg_devices, chan_devices - depth)
    first = jnp.maximum(first, 0)
    window = (first[:, None] + jnp.arange(depth, dtype=jnp.int32)[None, :]) * seg_devices + lanes[:, None]
    wanted = (window[:, :, None] * OFFBINS + jnp.arange(OFFBINS, dtype=jnp.int32)).reshape(-1)
    hit = wanted[:, None] == labels[None, :]
    onehot = jnp.where(hit, jnp.tile(weight, chan_count)[None, :], 0.0).astype(jnp.bfloat16)
    high = lax.reduce_precision(product, exponent_bits=8, mantissa_bits=7)
    low = product - high
    split = jnp.concatenate([high, low], axis=1).astype(jnp.bfloat16)
    both = jnp.dot(onehot, split, preferred_element_type=jnp.float32)
    edge_high = lax.reduce_precision(edge, exponent_bits=8, mantissa_bits=7)
    ends = jnp.concatenate([edge_high, edge - edge_high], axis=1).astype(jnp.bfloat16)
    tail = jnp.dot(onehot, ends, preferred_element_type=jnp.float32)
    direct = both[:, :LAGS] + both[:, LAGS:]
    mirror = jnp.concatenate([tail[:, :1] + tail[:, 1:], jnp.flip(direct[:, 1:], axis=1)], axis=1)
    total = direct + mirror
    scale = 1.0 / math.sqrt(traces.shape[2] * traces.shape[1] * seg_devices)
    stacked = (total * scale).reshape(seg_devices, depth * OFFBINS, LAGS)
    part = jnp.sum(lax.all_to_all(stacked, "seg", 0, 0, tiled=True), axis=0)
    own_first = first[lax.axis_index("seg")]
    dense = jnp.zeros((chan_devices, OFFBINS, LAGS), jnp.float32)
    dense = lax.dynamic_update_slice(dense, part.reshape(depth, OFFBINS, LAGS), (own_first, 0, 0))
    pieces = lax.all_to_all(dense, "chan", 0, 0, tiled=True)
    return jnp.sum(pieces, axis=0, keepdims=True)


def solution(mesh):
    placed = (P("chan", "seg", None), P("chan"), P("chan", None), P("chan", None))
    return jax.shard_map(
        shards,
        mesh=mesh,
        in_specs=placed,
        out_specs=P(("chan", "seg"), None, None),
        check_vma=False,
    )
```

```python
import math

import jax
import jax.numpy as jnp
from jax import lax
from jax.sharding import PartitionSpec as P

LAGS = 256
OFFBINS = 2


def normalize(traces, taper_len):
    values = traces.astype(jnp.float32)
    sample_count = values.shape[2]
    power = jnp.mean(values * values, axis=2, keepdims=True)
    times = jnp.arange(sample_count).astype(jnp.float32)
    length = taper_len.astype(jnp.float32)[:, None, None]
    window = jnp.minimum(1.0, jnp.minimum((times + 1.0) / length, (sample_count - times) / length))
    return (window * values * lax.rsqrt(power + 1e-06)).astype(jnp.bfloat16)


def toeplitz(normed, lag_count):
    chan_count, seg_count, sample_count = normed.shape
    flat = normed.reshape(chan_count, sample_count)
    half = lag_count // 2
    width = sample_count + lag_count + 1
    ring = jnp.concatenate(
        [flat[:, half:], jnp.zeros((chan_count, width - sample_count), flat.dtype), flat[:, :half]], axis=1
    )
    tiled = jnp.tile(ring, (1, lag_count + 1))[:, : lag_count * (width - 1)]
    return tiled.reshape(chan_count, lag_count, width - 1)[:, :, :sample_count]


def shards(traces, taper_len, gather_id, offset_bin):
    chan_count = traces.shape[0]
    chan_devices = lax.axis_size("chan")
    seg_devices = lax.axis_size("seg")
    bucket_count = chan_devices * seg_devices * OFFBINS
    normed = normalize(traces, taper_len)
    kernel = toeplitz(normed, LAGS)
    first_row = lax.axis_index("chan") * chan_count
    own_rows = first_row + jnp.arange(chan_count, dtype=jnp.int32)[None, :]
    flat = lax.optimization_barrier(normed.reshape(chan_count, -1))
    copies = jnp.broadcast_to(flat[None], (chan_devices,) + flat.shape)
    piece = lax.all_to_all(copies, "chan", 0, 0, tiled=True).reshape(-1, flat.shape[1])
    row_count = piece.shape[0]
    sample_count = piece.shape[1]
    me = lax.axis_index("chan")
    half = chan_devices // 2
    take = (half + 1) * chan_count
    near = lax.dynamic_slice(jnp.concatenate([piece, piece], axis=0), (me * chan_count, 0), (take, sample_count))
    block_of = jnp.arange(half + 1, dtype=jnp.int32)
    weight = jnp.where(block_of == 0, 0.5, 1.0)
    weight = jnp.where((block_of == half) & (me >= half), 0.0, weight)
    weight = jnp.repeat(weight, chan_count)
    product = jnp.einsum("it,jkt->ijk", near, kernel, preferred_element_type=jnp.float32)
    product = jnp.transpose(product, (1, 0, 2)).reshape(take * chan_count, LAGS)
    late = jnp.concatenate([jnp.zeros((chan_count, LAGS // 2), flat.dtype), flat[:, : sample_count - LAGS // 2]], axis=1)
    edge = jnp.einsum("it,jt->ji", near, late, preferred_element_type=jnp.float32).reshape(-1, 1)
    labels = gather_id * OFFBINS + offset_bin
    labels = lax.dynamic_slice(jnp.concatenate([labels, labels], axis=1), (0, me * chan_count), (chan_count, take))
    partner = jnp.arange(take, dtype=jnp.int32)[None, :]
    labels = jnp.where(partner == jnp.arange(chan_count, dtype=jnp.int32)[:, None], -1, labels).reshape(-1)
    gathers = chan_devices * seg_devices
    low_span = 2 * (row_count - 1)
    reach = (low_span + 5 * (chan_count - 1)) * gathers // (2 * low_span + 1) + 2
    depth = -(-(reach - 1) // seg_devices) + 1
    depth = -(-depth * OFFBINS // 8) * 8 // OFFBINS
    start = gather_id[0, 0]
    lanes = jnp.arange(seg_devices, dtype=jnp.int32)
    first = jnp.minimum((start - lanes + seg_devices - 1) // seg_devices, chan_devices - depth)
    first = jnp.maximum(first, 0)
    window = (first[:, None] + jnp.arange(depth, dtype=jnp.int32)[None, :]) * seg_devices + lanes[:, None]
    wanted = (window[:, :, None] * OFFBINS + jnp.arange(OFFBINS, dtype=jnp.int32)).reshape(-1)
    hit = wanted[:, None] == labels[None, :]
    onehot = jnp.where(hit, jnp.tile(weight, chan_count)[None, :], 0.0).astype(jnp.bfloat16)
    high = lax.reduce_precision(product, exponent_bits=8, mantissa_bits=7)
    low = product - high
    split = jnp.concatenate([high, low], axis=1).astype(jnp.bfloat16)
    both = jnp.dot(onehot, split, preferred_element_type=jnp.float32)
    edge_high = lax.reduce_precision(edge, exponent_bits=8, mantissa_bits=7)
    ends = jnp.concatenate([edge_high, edge - edge_high], axis=1).astype(jnp.bfloat16)
    tail = jnp.dot(onehot, ends, preferred_element_type=jnp.float32)
    direct = both[:, :LAGS] + both[:, LAGS:]
    first_lag = jnp.arange(LAGS, dtype=jnp.int32)[None, :] == 0
    total = direct + jnp.where(first_lag, tail[:, :1] + tail[:, 1:], 0.0)
    scale = 1.0 / math.sqrt(traces.shape[2] * traces.shape[1] * seg_devices)
    stacked = (total * scale).reshape(seg_devices, depth * OFFBINS, LAGS)
    part = jnp.sum(lax.all_to_all(stacked, "seg", 0, 0, tiled=True), axis=0)
    own_first = first[lax.axis_index("seg")]
    dense = jnp.zeros((chan_devices, OFFBINS, LAGS), jnp.float32)
    dense = lax.dynamic_update_slice(dense, part.reshape(depth, OFFBINS, LAGS), (own_first, 0, 0))
    pieces = lax.all_to_all(dense, "chan", 0, 0, tiled=True)
    summed = jnp.sum(pieces, axis=0, keepdims=True)
    flipped = jnp.flip(summed[:, :, 1:], axis=2)
    return summed + jnp.concatenate([jnp.zeros_like(summed[:, :, :1]), flipped], axis=2)


def solution(mesh):
    placed = (P("chan", "seg", None), P("chan"), P("chan", None), P("chan", None))
    return jax.shard_map(
        shards,
        mesh=mesh,
        in_specs=placed,
        out_specs=P(("chan", "seg"), None, None),
        check_vma=False,
    )
```

```python
import math

import jax
import jax.numpy as jnp
from jax import lax
from jax.sharding import PartitionSpec as P

LAGS = 256
OFFBINS = 2


def normalize(traces, taper_len):
    values = traces.astype(jnp.float32)
    sample_count = values.shape[2]
    power = jnp.mean(values * values, axis=2, keepdims=True)
    times = jnp.arange(sample_count).astype(jnp.float32)
    length = taper_len.astype(jnp.float32)[:, None, None]
    window = jnp.minimum(1.0, jnp.minimum((times + 1.0) / length, (sample_count - times) / length))
    return (window * values * lax.rsqrt(power + 1e-06)).astype(jnp.bfloat16)


def toeplitz(normed, lag_count):
    chan_count, seg_count, sample_count = normed.shape
    flat = normed.reshape(chan_count, sample_count)
    half = lag_count // 2
    width = sample_count + lag_count + 1
    ring = jnp.concatenate(
        [flat[:, half:], jnp.zeros((chan_count, width - sample_count), flat.dtype), flat[:, :half]], axis=1
    )
    tiled = jnp.tile(ring, (1, lag_count + 1))[:, : lag_count * (width - 1)]
    return tiled.reshape(chan_count, lag_count, width - 1)[:, :, :sample_count]


def shards(traces, taper_len, gather_id, offset_bin):
    chan_count = traces.shape[0]
    chan_devices = lax.axis_size("chan")
    seg_devices = lax.axis_size("seg")
    bucket_count = chan_devices * seg_devices * OFFBINS
    normed = normalize(traces, taper_len)
    kernel = toeplitz(normed, LAGS)
    first_row = lax.axis_index("chan") * chan_count
    own_rows = first_row + jnp.arange(chan_count, dtype=jnp.int32)[None, :]
    flat = normed.reshape(chan_count, -1)
    raw = traces.reshape(chan_count, -1)
    lengths = jnp.zeros((chan_count, 128), raw.dtype).at[:, 0].set(taper_len.astype(raw.dtype))
    packed = jnp.concatenate([raw, lengths], axis=1)
    copies = jnp.broadcast_to(packed[None], (chan_devices,) + packed.shape)
    got = lax.all_to_all(copies, "chan", 0, 0, tiled=True).reshape(-1, packed.shape[1])
    piece = normalize(got[:, None, : raw.shape[1]], got[:, raw.shape[1]]).reshape(-1, raw.shape[1])
    row_count = piece.shape[0]
    sample_count = piece.shape[1]
    me = lax.axis_index("chan")
    half = chan_devices // 2
    take = (half + 1) * chan_count
    near = lax.dynamic_slice(jnp.concatenate([piece, piece], axis=0), (me * chan_count, 0), (take, sample_count))
    block_of = jnp.arange(half + 1, dtype=jnp.int32)
    weight = jnp.where(block_of == 0, 0.5, 1.0)
    weight = jnp.where((block_of == half) & (me >= half), 0.0, weight)
    weight = jnp.repeat(weight, chan_count)
    product = jnp.einsum("it,jkt->ijk", near, kernel, preferred_element_type=jnp.float32)
    product = jnp.transpose(product, (1, 0, 2)).reshape(take * chan_count, LAGS)
    late = jnp.concatenate([jnp.zeros((chan_count, LAGS // 2), flat.dtype), flat[:, : sample_count - LAGS // 2]], axis=1)
    edge = jnp.einsum("it,jt->ji", near, late, preferred_element_type=jnp.float32).reshape(-1, 1)
    labels = gather_id * OFFBINS + offset_bin
    labels = lax.dynamic_slice(jnp.concatenate([labels, labels], axis=1), (0, me * chan_count), (chan_count, take))
    partner = jnp.arange(take, dtype=jnp.int32)[None, :]
    labels = jnp.where(partner == jnp.arange(chan_count, dtype=jnp.int32)[:, None], -1, labels).reshape(-1)
    gathers = chan_devices * seg_devices
    low_span = 2 * (row_count - 1)
    reach = (low_span + 5 * (chan_count - 1)) * gathers // (2 * low_span + 1) + 2
    depth = -(-(reach - 1) // seg_devices) + 1
    depth = -(-depth * OFFBINS // 8) * 8 // OFFBINS
    start = gather_id[0, 0]
    lanes = jnp.arange(seg_devices, dtype=jnp.int32)
    first = jnp.minimum((start - lanes + seg_devices - 1) // seg_devices, chan_devices - depth)
    first = jnp.maximum(first, 0)
    window = (first[:, None] + jnp.arange(depth, dtype=jnp.int32)[None, :]) * seg_devices + lanes[:, None]
    wanted = (window[:, :, None] * OFFBINS + jnp.arange(OFFBINS, dtype=jnp.int32)).reshape(-1)
    hit = wanted[:, None] == labels[None, :]
    onehot = jnp.where(hit, jnp.tile(weight, chan_count)[None, :], 0.0).astype(jnp.bfloat16)
    high = lax.reduce_precision(product, exponent_bits=8, mantissa_bits=7)
    low = product - high
    split = jnp.concatenate([high, low], axis=1).astype(jnp.bfloat16)
    both = jnp.dot(onehot, split, preferred_element_type=jnp.float32)
    edge_high = lax.reduce_precision(edge, exponent_bits=8, mantissa_bits=7)
    ends = jnp.concatenate([edge_high, edge - edge_high], axis=1).astype(jnp.bfloat16)
    tail = jnp.dot(onehot, ends, preferred_element_type=jnp.float32)
    direct = both[:, :LAGS] + both[:, LAGS:]
    first_lag = jnp.arange(LAGS, dtype=jnp.int32)[None, :] == 0
    total = direct + jnp.where(first_lag, tail[:, :1] + tail[:, 1:], 0.0)
    scale = 1.0 / math.sqrt(traces.shape[2] * traces.shape[1] * seg_devices)
    stacked = (total * scale).reshape(seg_devices, depth * OFFBINS, LAGS)
    part = jnp.sum(lax.all_to_all(stacked, "seg", 0, 0, tiled=True), axis=0)
    own_first = first[lax.axis_index("seg")]
    dense = jnp.zeros((chan_devices, OFFBINS, LAGS), jnp.float32)
    dense = lax.dynamic_update_slice(dense, part.reshape(depth, OFFBINS, LAGS), (own_first, 0, 0))
    pieces = lax.all_to_all(dense, "chan", 0, 0, tiled=True)
    summed = jnp.sum(pieces, axis=0, keepdims=True)
    flipped = jnp.flip(summed[:, :, 1:], axis=2)
    return summed + jnp.concatenate([jnp.zeros_like(summed[:, :, :1]), flipped], axis=2)


def solution(mesh):
    placed = (P("chan", "seg", None), P("chan"), P("chan", None), P("chan", None))
    return jax.shard_map(
        shards,
        mesh=mesh,
        in_specs=placed,
        out_specs=P(("chan", "seg"), None, None),
        check_vma=False,
    )
```

```python
import math

import jax
import jax.numpy as jnp
from jax import lax
from jax.sharding import PartitionSpec as P

LAGS = 256
OFFBINS = 2


def normalize(traces, taper_len):
    values = traces.astype(jnp.float32)
    sample_count = values.shape[2]
    power = jnp.mean(values * values, axis=2, keepdims=True)
    times = jnp.arange(sample_count).astype(jnp.float32)
    length = taper_len.astype(jnp.float32)[:, None, None]
    window = jnp.minimum(1.0, jnp.minimum((times + 1.0) / length, (sample_count - times) / length))
    return (window * values * lax.rsqrt(power + 1e-06)).astype(jnp.bfloat16)


def toeplitz(normed, lag_count):
    chan_count, seg_count, sample_count = normed.shape
    flat = normed.reshape(chan_count, sample_count)
    half = lag_count // 2
    width = sample_count + lag_count + 1
    ring = jnp.concatenate(
        [flat[:, half:], jnp.zeros((chan_count, width - sample_count), flat.dtype), flat[:, :half]], axis=1
    )
    tiled = jnp.tile(ring, (1, lag_count + 1))[:, : lag_count * (width - 1)]
    return tiled.reshape(chan_count, lag_count, width - 1)[:, :, :sample_count]


def shards(traces, taper_len, gather_id, offset_bin):
    chan_count = traces.shape[0]
    chan_devices = lax.axis_size("chan")
    seg_devices = lax.axis_size("seg")
    bucket_count = chan_devices * seg_devices * OFFBINS
    normed = normalize(traces, taper_len)
    kernel = toeplitz(normed, LAGS)
    first_row = lax.axis_index("chan") * chan_count
    own_rows = first_row + jnp.arange(chan_count, dtype=jnp.int32)[None, :]
    flat = lax.optimization_barrier(normed.reshape(chan_count, -1))
    copies = jnp.broadcast_to(flat[None], (chan_devices,) + flat.shape)
    piece = lax.all_to_all(copies, "chan", 0, 0, tiled=True).reshape(-1, flat.shape[1])
    row_count = piece.shape[0]
    sample_count = piece.shape[1]
    me = lax.axis_index("chan")
    half = chan_devices // 2
    take = (half + 1) * chan_count
    near = lax.dynamic_slice(jnp.concatenate([piece, piece], axis=0), (me * chan_count, 0), (take, sample_count))
    block_of = jnp.arange(half + 1, dtype=jnp.int32)
    weight = jnp.where(block_of == 0, 0.5, 1.0)
    weight = jnp.where((block_of == half) & (me >= half), 0.0, weight)
    weight = jnp.repeat(weight, chan_count)
    product = jnp.einsum("it,jkt->ijk", near, kernel, preferred_element_type=jnp.float32)
    product = jnp.transpose(product, (1, 0, 2)).reshape(take * chan_count, LAGS)
    late = jnp.concatenate([jnp.zeros((chan_count, LAGS // 2), flat.dtype), flat[:, : sample_count - LAGS // 2]], axis=1)
    edge = jnp.einsum("it,jt->ji", near, late, preferred_element_type=jnp.float32).reshape(-1, 1)
    labels = gather_id * OFFBINS + offset_bin
    labels = lax.dynamic_slice(jnp.concatenate([labels, labels], axis=1), (0, me * chan_count), (chan_count, take))
    partner = jnp.arange(take, dtype=jnp.int32)[None, :]
    labels = jnp.where(partner == jnp.arange(chan_count, dtype=jnp.int32)[:, None], -1, labels).reshape(-1)
    gathers = chan_devices * seg_devices
    low_span = 2 * (row_count - 1)
    reach = (low_span + 5 * (chan_count - 1)) * gathers // (2 * low_span + 1) + 2
    depth = -(-(reach - 1) // seg_devices) + 1
    depth = -(-depth * OFFBINS // 8) * 8 // OFFBINS
    start = gather_id[0, 0]
    lanes = jnp.arange(seg_devices, dtype=jnp.int32)
    first = jnp.minimum((start - lanes + seg_devices - 1) // seg_devices, chan_devices - depth)
    first = jnp.maximum(first, 0)
    window = (first[:, None] + jnp.arange(depth, dtype=jnp.int32)[None, :]) * seg_devices + lanes[:, None]
    wanted = (window[:, :, None] * OFFBINS + jnp.arange(OFFBINS, dtype=jnp.int32)).reshape(-1)
    hit = wanted[:, None] == labels[None, :]
    onehot = jnp.where(hit, jnp.tile(weight, chan_count)[None, :], 0.0)
    direct = jnp.dot(onehot, product, precision=lax.Precision.HIGH, preferred_element_type=jnp.float32)
    tail = jnp.dot(onehot, edge, precision=lax.Precision.HIGH, preferred_element_type=jnp.float32)
    mirror = jnp.concatenate([tail, jnp.flip(direct[:, 1:], axis=1)], axis=1)
    total = direct + mirror
    scale = 1.0 / math.sqrt(traces.shape[2] * traces.shape[1] * seg_devices)
    stacked = (total * scale).reshape(seg_devices, depth * OFFBINS, LAGS)
    part = jnp.sum(lax.all_to_all(stacked, "seg", 0, 0, tiled=True), axis=0)
    own_first = first[lax.axis_index("seg")]
    dense = jnp.zeros((chan_devices, OFFBINS, LAGS), jnp.float32)
    dense = lax.dynamic_update_slice(dense, part.reshape(depth, OFFBINS, LAGS), (own_first, 0, 0))
    pieces = lax.all_to_all(dense, "chan", 0, 0, tiled=True)
    return jnp.sum(pieces, axis=0, keepdims=True)


def solution(mesh):
    placed = (P("chan", "seg", None), P("chan"), P("chan", None), P("chan", None))
    return jax.shard_map(
        shards,
        mesh=mesh,
        in_specs=placed,
        out_specs=P(("chan", "seg"), None, None),
        check_vma=False,
    )
```

```python
import math

import jax
import jax.numpy as jnp
from jax import lax
from jax.sharding import PartitionSpec as P

LAGS = 256
OFFBINS = 2


def normalize(traces, taper_len):
    values = traces.astype(jnp.float32)
    sample_count = values.shape[2]
    power = jnp.mean(values * values, axis=2, keepdims=True)
    times = jnp.arange(sample_count).astype(jnp.float32)
    length = taper_len.astype(jnp.float32)[:, None, None]
    window = jnp.minimum(1.0, jnp.minimum((times + 1.0) / length, (sample_count - times) / length))
    return (window * values * lax.rsqrt(power + 1e-06)).astype(jnp.bfloat16)


def toeplitz(normed, lag_count):
    chan_count, seg_count, sample_count = normed.shape
    flat = normed.reshape(chan_count, sample_count)
    half = lag_count // 2
    width = sample_count + lag_count + 1
    ring = jnp.concatenate(
        [flat[:, half:], jnp.zeros((chan_count, width - sample_count), flat.dtype), flat[:, :half]], axis=1
    )
    tiled = jnp.tile(ring, (1, lag_count + 1))[:, : lag_count * (width - 1)]
    return tiled.reshape(chan_count, lag_count, width - 1)[:, :, :sample_count]


def shards(traces, taper_len, gather_id, offset_bin):
    chan_count = traces.shape[0]
    chan_devices = lax.axis_size("chan")
    seg_devices = lax.axis_size("seg")
    bucket_count = chan_devices * seg_devices * OFFBINS
    normed = normalize(traces, taper_len)
    kernel = toeplitz(normed, LAGS)
    first_row = lax.axis_index("chan") * chan_count
    own_rows = first_row + jnp.arange(chan_count, dtype=jnp.int32)[None, :]
    flat = lax.optimization_barrier(normed.reshape(chan_count, -1))
    copies = jnp.broadcast_to(flat[None], (chan_devices,) + flat.shape)
    piece = lax.all_to_all(copies, "chan", 0, 0, tiled=True).reshape(-1, flat.shape[1])
    row_count = piece.shape[0]
    sample_count = piece.shape[1]
    me = lax.axis_index("chan")
    half = chan_devices // 2
    take = (half + 1) * chan_count
    near = lax.dynamic_slice(jnp.concatenate([piece, piece], axis=0), (me * chan_count, 0), (take, sample_count))
    block_of = jnp.arange(half + 1, dtype=jnp.int32)
    weight = jnp.where(block_of == 0, 0.5, 1.0)
    weight = jnp.where((block_of == half) & (me >= half), 0.0, weight)
    weight = jnp.repeat(weight, chan_count)
    product = jnp.einsum("it,jkt->ijk", near, kernel, preferred_element_type=jnp.float32)
    product = jnp.transpose(product, (1, 0, 2)).reshape(take * chan_count, LAGS)
    late = jnp.concatenate([jnp.zeros((chan_count, LAGS // 2), flat.dtype), flat[:, : sample_count - LAGS // 2]], axis=1)
    edge = jnp.einsum("it,jt->ji", near, late, preferred_element_type=jnp.float32).reshape(-1, 1)
    labels = gather_id * OFFBINS + offset_bin
    labels = lax.dynamic_slice(jnp.concatenate([labels, labels], axis=1), (0, me * chan_count), (chan_count, take))
    partner = jnp.arange(take, dtype=jnp.int32)[None, :]
    labels = jnp.where(partner == jnp.arange(chan_count, dtype=jnp.int32)[:, None], -1, labels).reshape(-1)
    gathers = chan_devices * seg_devices
    low_span = 2 * (row_count - 1)
    reach = (low_span + 5 * (chan_count - 1)) * gathers // (2 * low_span + 1) + 2
    depth = -(-(reach - 1) // seg_devices) + 1
    depth = -(-depth * OFFBINS // 8) * 8 // OFFBINS
    start = gather_id[0, 0]
    lanes = jnp.arange(seg_devices, dtype=jnp.int32)
    first = jnp.minimum((start - lanes + seg_devices - 1) // seg_devices, chan_devices - depth)
    first = jnp.maximum(first, 0)
    window = (first[:, None] + jnp.arange(depth, dtype=jnp.int32)[None, :]) * seg_devices + lanes[:, None]
    wanted = (window[:, :, None] * OFFBINS + jnp.arange(OFFBINS, dtype=jnp.int32)).reshape(-1)
    hit = wanted[:, None] == labels[None, :]
    onehot = jnp.where(hit, jnp.tile(weight, chan_count)[None, :], 0.0).astype(jnp.bfloat16)
    high = lax.reduce_precision(product, exponent_bits=8, mantissa_bits=7)
    low = product - high
    split = jnp.concatenate([high, low], axis=1).astype(jnp.bfloat16)
    both = jnp.dot(onehot, split, preferred_element_type=jnp.float32)
    edge_high = lax.reduce_precision(edge, exponent_bits=8, mantissa_bits=7)
    ends = jnp.concatenate([edge_high, edge - edge_high], axis=1).astype(jnp.bfloat16)
    tail = jnp.dot(onehot, ends, preferred_element_type=jnp.float32)
    direct = both[:, :LAGS] + both[:, LAGS:]
    mirror = jnp.concatenate([tail[:, :1] + tail[:, 1:], jnp.flip(direct[:, 1:], axis=1)], axis=1)
    total = direct + mirror
    scale = 1.0 / math.sqrt(traces.shape[2] * traces.shape[1] * seg_devices)
    stacked = (total * scale).reshape(seg_devices, depth * OFFBINS, LAGS)
    part = jnp.sum(lax.all_to_all(stacked, "seg", 0, 0, tiled=True), axis=0)
    own_first = first[lax.axis_index("seg")]
    dense = jnp.zeros((chan_devices, OFFBINS, LAGS), jnp.float32)
    dense = lax.dynamic_update_slice(dense, part.reshape(depth, OFFBINS, LAGS), (own_first, 0, 0))
    tiles = dense.reshape(chan_devices, OFFBINS * LAGS // 128, 128)
    pieces = lax.all_to_all(tiles, "chan", 0, 0, tiled=True)
    return jnp.sum(pieces, axis=0).reshape(1, OFFBINS, LAGS)


def solution(mesh):
    placed = (P("chan", "seg", None), P("chan"), P("chan", None), P("chan", None))
    return jax.shard_map(
        shards,
        mesh=mesh,
        in_specs=placed,
        out_specs=P(("chan", "seg"), None, None),
        check_vma=False,
    )
```

```python
import math

import jax
import jax.numpy as jnp
from jax import lax
from jax.sharding import PartitionSpec as P

LAGS = 256
OFFBINS = 2


def normalize(traces, taper_len):
    values = traces.astype(jnp.float32)
    sample_count = values.shape[2]
    power = jnp.mean(values * values, axis=2, keepdims=True)
    times = jnp.arange(sample_count).astype(jnp.float32)
    length = taper_len.astype(jnp.float32)[:, None, None]
    window = jnp.minimum(1.0, jnp.minimum((times + 1.0) / length, (sample_count - times) / length))
    return (window * values * lax.rsqrt(power + 1e-06)).astype(jnp.bfloat16)


def toeplitz(normed, lag_count):
    chan_count, seg_count, sample_count = normed.shape
    flat = normed.reshape(chan_count, sample_count)
    half = lag_count // 2
    width = sample_count + lag_count + 1
    ring = jnp.concatenate(
        [flat[:, half:], jnp.zeros((chan_count, width - sample_count), flat.dtype), flat[:, :half]], axis=1
    )
    tiled = jnp.tile(ring, (1, lag_count + 1))[:, : lag_count * (width - 1)]
    return tiled.reshape(chan_count, lag_count, width - 1)[:, :, :sample_count]


def shards(traces, taper_len, gather_id, offset_bin):
    chan_count = traces.shape[0]
    chan_devices = lax.axis_size("chan")
    seg_devices = lax.axis_size("seg")
    bucket_count = chan_devices * seg_devices * OFFBINS
    normed = normalize(traces, taper_len)
    kernel = toeplitz(normed, LAGS)
    first_row = lax.axis_index("chan") * chan_count
    own_rows = first_row + jnp.arange(chan_count, dtype=jnp.int32)[None, :]
    flat = lax.optimization_barrier(normed.reshape(chan_count, -1))
    copies = jnp.broadcast_to(flat[None], (chan_devices,) + flat.shape)
    piece = lax.all_to_all(copies, "chan", 0, 0, tiled=True).reshape(-1, flat.shape[1])
    row_count = piece.shape[0]
    sample_count = piece.shape[1]
    me = lax.axis_index("chan")
    half = chan_devices // 2
    take = (half + 1) * chan_count
    near = lax.dynamic_slice(jnp.concatenate([piece, piece], axis=0), (me * chan_count, 0), (take, sample_count))
    block_of = jnp.arange(half + 1, dtype=jnp.int32)
    weight = jnp.where(block_of == 0, 0.5, 1.0)
    weight = jnp.where((block_of == half) & (me >= half), 0.0, weight)
    weight = jnp.repeat(weight, chan_count)
    product = jnp.einsum("it,jkt->ijk", near, kernel, preferred_element_type=jnp.float32)
    product = jnp.transpose(product, (1, 0, 2)).reshape(take * chan_count, LAGS)
    late = jnp.concatenate([jnp.zeros((chan_count, LAGS // 2), flat.dtype), flat[:, : sample_count - LAGS // 2]], axis=1)
    edge = jnp.einsum("it,jt->ji", near, late, preferred_element_type=jnp.float32).reshape(-1, 1)
    labels = gather_id * OFFBINS + offset_bin
    labels = lax.dynamic_slice(jnp.concatenate([labels, labels], axis=1), (0, me * chan_count), (chan_count, take))
    partner = jnp.arange(take, dtype=jnp.int32)[None, :]
    labels = jnp.where(partner == jnp.arange(chan_count, dtype=jnp.int32)[:, None], -1, labels).reshape(-1)
    gathers = chan_devices * seg_devices
    low_span = 2 * (row_count - 1)
    reach = (low_span + 5 * (chan_count - 1)) * gathers // (2 * low_span + 1) + 2
    depth = -(-(reach - 1) // seg_devices) + 1
    depth = -(-depth * OFFBINS // 8) * 8 // OFFBINS
    start = gather_id[0, 0]
    lanes = jnp.arange(seg_devices, dtype=jnp.int32)
    first = jnp.minimum((start - lanes + seg_devices - 1) // seg_devices, chan_devices - depth)
    first = jnp.maximum(first, 0)
    window = (first[:, None] + jnp.arange(depth, dtype=jnp.int32)[None, :]) * seg_devices + lanes[:, None]
    wanted = (window[:, :, None] * OFFBINS + jnp.arange(OFFBINS, dtype=jnp.int32)).reshape(-1)
    hit = wanted[:, None] == labels[None, :]
    onehot = jnp.where(hit, jnp.tile(weight, chan_count)[None, :], 0.0).astype(jnp.bfloat16)
    high = lax.reduce_precision(product, exponent_bits=8, mantissa_bits=7)
    low = product - high
    split = jnp.concatenate([high, low], axis=1).astype(jnp.bfloat16)
    both = jnp.dot(onehot, split, preferred_element_type=jnp.float32)
    edge_high = lax.reduce_precision(edge, exponent_bits=8, mantissa_bits=7)
    ends = jnp.concatenate([edge_high, edge - edge_high], axis=1).astype(jnp.bfloat16)
    tail = jnp.dot(onehot, ends, preferred_element_type=jnp.float32)
    direct = both[:, :LAGS] + both[:, LAGS:]
    first_lag = jnp.arange(LAGS, dtype=jnp.int32)[None, :] == 0
    total = direct + jnp.where(first_lag, tail[:, :1] + tail[:, 1:], 0.0)
    scale = 1.0 / math.sqrt(traces.shape[2] * traces.shape[1] * seg_devices)
    stacked = (total * scale).reshape(seg_devices, depth * OFFBINS, LAGS)
    part = jnp.sum(lax.all_to_all(stacked, "seg", 0, 0, tiled=True), axis=0)
    own_first = first[lax.axis_index("seg")]
    dense = jnp.zeros((chan_devices, OFFBINS, LAGS), jnp.float32)
    dense = lax.dynamic_update_slice(dense, part.reshape(depth, OFFBINS, LAGS), (own_first, 0, 0))
    tiles = dense.reshape(chan_devices, OFFBINS * LAGS // 128, 128)
    pieces = lax.all_to_all(tiles, "chan", 0, 0, tiled=True)
    summed = jnp.sum(pieces, axis=0).reshape(1, OFFBINS, LAGS)
    flipped = jnp.flip(summed[:, :, 1:], axis=2)
    return summed + jnp.concatenate([jnp.zeros_like(summed[:, :, :1]), flipped], axis=2)


def solution(mesh):
    placed = (P("chan", "seg", None), P("chan"), P("chan", None), P("chan", None))
    return jax.shard_map(
        shards,
        mesh=mesh,
        in_specs=placed,
        out_specs=P(("chan", "seg"), None, None),
        check_vma=False,
    )
```

```python
import math

import jax
import jax.numpy as jnp
from jax import lax
from jax.sharding import PartitionSpec as P

LAGS = 256
OFFBINS = 2


def normalize(traces, taper_len):
    values = traces.astype(jnp.float32)
    sample_count = values.shape[2]
    power = jnp.mean(values * values, axis=2, keepdims=True)
    times = jnp.arange(sample_count).astype(jnp.float32)
    length = taper_len.astype(jnp.float32)[:, None, None]
    window = jnp.minimum(1.0, jnp.minimum((times + 1.0) / length, (sample_count - times) / length))
    return (window * values * lax.rsqrt(power + 1e-06)).astype(jnp.bfloat16)


def toeplitz(normed, lag_count):
    chan_count, seg_count, sample_count = normed.shape
    flat = normed.reshape(chan_count, sample_count)
    half = lag_count // 2
    width = sample_count + lag_count + 1
    ring = jnp.concatenate(
        [flat[:, half:], jnp.zeros((chan_count, width - sample_count), flat.dtype), flat[:, :half]], axis=1
    )
    tiled = jnp.tile(ring, (1, lag_count + 1))[:, : lag_count * (width - 1)]
    return tiled.reshape(chan_count, lag_count, width - 1)[:, :, :sample_count]


def shards(traces, taper_len, gather_id, offset_bin):
    chan_count = traces.shape[0]
    chan_devices = lax.axis_size("chan")
    seg_devices = lax.axis_size("seg")
    bucket_count = chan_devices * seg_devices * OFFBINS
    normed = normalize(traces, taper_len)
    kernel = toeplitz(normed, LAGS)
    first_row = lax.axis_index("chan") * chan_count
    own_rows = first_row + jnp.arange(chan_count, dtype=jnp.int32)[None, :]
    flat = normed.reshape(chan_count, -1)
    copies = jnp.broadcast_to(flat[None], (chan_devices,) + flat.shape)
    piece = lax.all_to_all(copies, "chan", 0, 0, tiled=True).reshape(-1, flat.shape[1])
    row_count = piece.shape[0]
    sample_count = piece.shape[1]
    me = lax.axis_index("chan")
    half = chan_devices // 2
    take = (half + 1) * chan_count
    near = lax.dynamic_slice(jnp.concatenate([piece, piece], axis=0), (me * chan_count, 0), (take, sample_count))
    block_of = jnp.arange(half + 1, dtype=jnp.int32)
    weight = jnp.where(block_of == 0, 0.5, 1.0)
    weight = jnp.where((block_of == half) & (me >= half), 0.0, weight)
    weight = jnp.repeat(weight, chan_count)
    product = jnp.einsum("it,jkt->ijk", near, kernel, preferred_element_type=jnp.float32)
    product = jnp.transpose(product, (1, 0, 2)).reshape(take * chan_count, LAGS)
    late = jnp.concatenate([jnp.zeros((chan_count, LAGS // 2), flat.dtype), flat[:, : sample_count - LAGS // 2]], axis=1)
    edge = jnp.einsum("it,jt->ji", near, late, preferred_element_type=jnp.float32).reshape(-1, 1)
    labels = gather_id * OFFBINS + offset_bin
    labels = lax.dynamic_slice(jnp.concatenate([labels, labels], axis=1), (0, me * chan_count), (chan_count, take))
    partner = jnp.arange(take, dtype=jnp.int32)[None, :]
    labels = jnp.where(partner == jnp.arange(chan_count, dtype=jnp.int32)[:, None], -1, labels).reshape(-1)
    gathers = chan_devices * seg_devices
    low_span = 2 * (row_count - 1)
    reach = (low_span + 5 * (chan_count - 1)) * gathers // (2 * low_span + 1) + 2
    depth = -(-(reach - 1) // seg_devices) + 1
    depth = -(-depth * OFFBINS // 8) * 8 // OFFBINS
    start = gather_id[0, 0]
    lanes = jnp.arange(seg_devices, dtype=jnp.int32)
    first = jnp.minimum((start - lanes + seg_devices - 1) // seg_devices, chan_devices - depth)
    first = jnp.maximum(first, 0)
    window = (first[:, None] + jnp.arange(depth, dtype=jnp.int32)[None, :]) * seg_devices + lanes[:, None]
    wanted = (window[:, :, None] * OFFBINS + jnp.arange(OFFBINS, dtype=jnp.int32)).reshape(-1)
    hit = wanted[:, None] == labels[None, :]
    onehot = jnp.where(hit, jnp.tile(weight, chan_count)[None, :], 0.0).astype(jnp.bfloat16)
    high = lax.reduce_precision(product, exponent_bits=8, mantissa_bits=7)
    low = product - high
    split = jnp.concatenate([high, low], axis=1).astype(jnp.bfloat16)
    both = jnp.dot(onehot, split, preferred_element_type=jnp.float32)
    edge_high = lax.reduce_precision(edge, exponent_bits=8, mantissa_bits=7)
    ends = jnp.concatenate([edge_high, edge - edge_high], axis=1).astype(jnp.bfloat16)
    tail = jnp.dot(onehot, ends, preferred_element_type=jnp.float32)
    direct = both[:, :LAGS] + both[:, LAGS:]
    mirror = jnp.concatenate([tail[:, :1] + tail[:, 1:], jnp.flip(direct[:, 1:], axis=1)], axis=1)
    total = direct + mirror
    scale = 1.0 / math.sqrt(traces.shape[2] * traces.shape[1] * seg_devices)
    stacked = (total * scale).reshape(seg_devices, depth * OFFBINS, LAGS)
    part = jnp.sum(lax.all_to_all(stacked, "seg", 0, 0, tiled=True), axis=0)
    own_first = first[lax.axis_index("seg")]
    dense = jnp.zeros((chan_devices, OFFBINS, LAGS), jnp.float32)
    dense = lax.dynamic_update_slice(dense, part.reshape(depth, OFFBINS, LAGS), (own_first, 0, 0))
    pieces = lax.all_to_all(dense, "chan", 0, 0, tiled=True)
    return jnp.sum(pieces, axis=0, keepdims=True)


def solution(mesh):
    placed = (P("chan", "seg", None), P("chan"), P("chan", None), P("chan", None))
    return jax.shard_map(
        shards,
        mesh=mesh,
        in_specs=placed,
        out_specs=P(("chan", "seg"), None, None),
        check_vma=False,
    )
```

```python
import math

import jax
import jax.numpy as jnp
from jax import lax
from jax.sharding import PartitionSpec as P

LAGS = 256
OFFBINS = 2


def normalize(traces, taper_len):
    values = traces.astype(jnp.float32)
    sample_count = values.shape[2]
    power = jnp.mean(values * values, axis=2, keepdims=True)
    times = jnp.arange(sample_count).astype(jnp.float32)
    length = taper_len.astype(jnp.float32)[:, None, None]
    window = jnp.minimum(1.0, jnp.minimum((times + 1.0) / length, (sample_count - times) / length))
    return (window * values * lax.rsqrt(power + 1e-06)).astype(jnp.bfloat16)


def toeplitz(normed, lag_count):
    chan_count, seg_count, sample_count = normed.shape
    flat = normed.reshape(chan_count, sample_count)
    half = lag_count // 2
    width = sample_count + lag_count + 1
    ring = jnp.concatenate(
        [flat[:, half:], jnp.zeros((chan_count, width - sample_count), flat.dtype), flat[:, :half]], axis=1
    )
    tiled = jnp.tile(ring, (1, lag_count + 1))[:, : lag_count * (width - 1)]
    return tiled.reshape(chan_count, lag_count, width - 1)[:, :, :sample_count]


def shards(traces, taper_len, gather_id, offset_bin):
    chan_count = traces.shape[0]
    chan_devices = lax.axis_size("chan")
    seg_devices = lax.axis_size("seg")
    bucket_count = chan_devices * seg_devices * OFFBINS
    normed = normalize(traces, taper_len)
    kernel = toeplitz(normed, LAGS)
    first_row = lax.axis_index("chan") * chan_count
    own_rows = first_row + jnp.arange(chan_count, dtype=jnp.int32)[None, :]
    flat = normed.reshape(chan_count, -1)
    copies = jnp.broadcast_to(flat[None], (chan_devices,) + flat.shape)
    piece = lax.all_to_all(copies, "chan", 0, 0, tiled=True).reshape(-1, flat.shape[1])
    row_count = piece.shape[0]
    sample_count = piece.shape[1]
    me = lax.axis_index("chan")
    half = chan_devices // 2
    take = (half + 1) * chan_count
    near = lax.dynamic_slice(jnp.concatenate([piece, piece], axis=0), (me * chan_count, 0), (take, sample_count))
    block_of = jnp.arange(half + 1, dtype=jnp.int32)
    weight = jnp.where(block_of == 0, 0.5, 1.0)
    weight = jnp.where((block_of == half) & (me >= half), 0.0, weight)
    weight = jnp.repeat(weight, chan_count)
    product = jnp.einsum("it,jkt->ijk", near, kernel, preferred_element_type=jnp.float32)
    product = jnp.transpose(product, (1, 0, 2)).reshape(take * chan_count, LAGS)
    late = jnp.concatenate([jnp.zeros((chan_count, LAGS // 2), flat.dtype), flat[:, : sample_count - LAGS // 2]], axis=1)
    edge = jnp.einsum("it,jt->ji", near, late, preferred_element_type=jnp.float32).reshape(-1, 1)
    labels = gather_id * OFFBINS + offset_bin
    labels = lax.dynamic_slice(jnp.concatenate([labels, labels], axis=1), (0, me * chan_count), (chan_count, take))
    partner = jnp.arange(take, dtype=jnp.int32)[None, :]
    labels = jnp.where(partner == jnp.arange(chan_count, dtype=jnp.int32)[:, None], -1, labels).reshape(-1)
    gathers = chan_devices * seg_devices
    low_span = 2 * (row_count - 1)
    reach = (low_span + 5 * (chan_count - 1)) * gathers // (2 * low_span + 1) + 2
    depth = -(-(reach - 1) // seg_devices) + 1
    depth = -(-depth * OFFBINS // 8) * 8 // OFFBINS
    start = gather_id[0, 0]
    lanes = jnp.arange(seg_devices, dtype=jnp.int32)
    first = jnp.minimum((start - lanes + seg_devices - 1) // seg_devices, chan_devices - depth)
    first = jnp.maximum(first, 0)
    window = (first[:, None] + jnp.arange(depth, dtype=jnp.int32)[None, :]) * seg_devices + lanes[:, None]
    wanted = (window[:, :, None] * OFFBINS + jnp.arange(OFFBINS, dtype=jnp.int32)).reshape(-1)
    hit = wanted[:, None] == labels[None, :]
    onehot = jnp.where(hit, jnp.tile(weight, chan_count)[None, :], 0.0).astype(jnp.bfloat16)
    high = lax.reduce_precision(product, exponent_bits=8, mantissa_bits=7)
    low = product - high
    split = jnp.concatenate([high, low], axis=1).astype(jnp.bfloat16)
    both = jnp.dot(onehot, split, preferred_element_type=jnp.float32)
    edge_high = lax.reduce_precision(edge, exponent_bits=8, mantissa_bits=7)
    ends = jnp.concatenate([edge_high, edge - edge_high], axis=1).astype(jnp.bfloat16)
    tail = jnp.dot(onehot, ends, preferred_element_type=jnp.float32)
    direct = both[:, :LAGS] + both[:, LAGS:]
    first_lag = jnp.arange(LAGS, dtype=jnp.int32)[None, :] == 0
    total = direct + jnp.where(first_lag, tail[:, :1] + tail[:, 1:], 0.0)
    scale = 1.0 / math.sqrt(traces.shape[2] * traces.shape[1] * seg_devices)
    stacked = (total * scale).reshape(seg_devices, depth * OFFBINS, LAGS)
    part = jnp.sum(lax.all_to_all(stacked, "seg", 0, 0, tiled=True), axis=0)
    own_first = first[lax.axis_index("seg")]
    dense = jnp.zeros((chan_devices, OFFBINS, LAGS), jnp.float32)
    dense = lax.dynamic_update_slice(dense, part.reshape(depth, OFFBINS, LAGS), (own_first, 0, 0))
    pieces = lax.all_to_all(dense, "chan", 0, 0, tiled=True)
    summed = jnp.sum(pieces, axis=0, keepdims=True)
    flipped = jnp.flip(summed[:, :, 1:], axis=2)
    return summed + jnp.concatenate([jnp.zeros_like(summed[:, :, :1]), flipped], axis=2)


def solution(mesh):
    placed = (P("chan", "seg", None), P("chan"), P("chan", None), P("chan", None))
    return jax.shard_map(
        shards,
        mesh=mesh,
        in_specs=placed,
        out_specs=P(("chan", "seg"), None, None),
        check_vma=False,
    )
```
